32 devices in a mesh: tok: 8 (over z, core), head: 4 (over y, x).
Axes of the slice: x: 2, y: 2, z: 4, core: 2. Of those that a mesh axis runs over, the one named last changes fastest.
Arguments:
- query_states: bfloat16 [12288, 3072], P('tok', 'head')
- key_states: bfloat16 [12288, 3072], P('tok', 'head')
- value_states: bfloat16 [12288, 3072], P('tok', 'head'), may hold values from -6 to 6
- query_gain: float32 [3072], P('head'), may hold values from 1 to 2.5
- key_gain: float32 [3072], P('head'), may hold values from 1 to 2.5
- windows: int32 [48, 27], P('tok'), may hold values from -1 to 47, as said below
Outputs:
- attention: bfloat16 [12288, 3072], P('tok', 'head')
The draws below stay inside these ranges and needn't reach their ends.
Inputs may be any that keep to these rules, and one draw needn't show every extreme that they name: Slots 0 to 8 of windows[i] name tiles of the tile-frame before tile i's, the next 9 tiles of its own tile-frame, the last 9 tiles of the tile-frame after it; in each group the named tiles come first and -1 fills the rest; tile i itself is always named; no tile is named twice in a row; a named tile's tile row and tile column differ from tile i's by at most 2 each, and some named tiles differ by 2 in both.
All inputs are finite; a program needn't handle non-finite values.
Results may differ from the reference program's by a relative error of at most 0.012.
The reference program's roundings to bfloat16 on the way count: a program that leaves them out, or rounds other values in their place, can miss the bound.
Values may be sent and summed in bfloat16 or wider, within the bound.
No kernel may reach another device: no remote copies, remote signals or barrier semaphores. Data moves between devices by JAX's collectives and lax.ppermute only.
A program may use at most 320 MiB of HBM per device.

```python
import math
import jax
import jax.numpy as jnp
from jax import lax

HEADS = 24
HEAD_DIM = 128
GRID_ROWS = 4
GRID_COLS = 4
FRAME_SLOTS = 9
MODEL_DIM = 3072
TILE_TOKENS = 256
WINDOW_SLOTS = 27
TILES = 48
GRID_FRAMES = 3
TOKENS = 12288


def joint_fields(key):
    streams = [jax.random.fold_in(key, 100 + number) for number in range(10)]
    column = jnp.arange(MODEL_DIM, dtype=jnp.float32) / (MODEL_DIM - 1)
    ramp = 3.0 ** (0.5 * column)
    query_base = jax.random.normal(streams[0], (TOKENS, MODEL_DIM), jnp.float32)
    key_base = jax.random.normal(streams[1], (TOKENS, MODEL_DIM), jnp.float32)
    query_cols = 10.0 ** jax.random.uniform(streams[2], (MODEL_DIM,), jnp.float32) * ramp
    key_cols = 10.0 ** jax.random.uniform(streams[3], (MODEL_DIM,), jnp.float32) * ramp
    query_rowscale = 10.0 ** jax.random.uniform(streams[4], (TOKENS, 1), jnp.float32)
    key_rowscale = 10.0 ** jax.random.uniform(streams[5], (TOKENS, 1), jnp.float32)
    queries = query_base * query_rowscale * query_cols[None, :]
    keyed = key_base * key_rowscale * key_cols[None, :]
    return (queries, keyed)


def draw_query_states(key, part):
    return joint_fields(key)[0].astype(jnp.bfloat16)


def draw_key_states(key, part):
    return joint_fields(key)[1].astype(jnp.bfloat16)


def draw_windows(key, part):
    tile_number = jnp.arange(TILES, dtype=jnp.int32)
    tile_frame = tile_number // (GRID_ROWS * GRID_COLS)
    tile_row = tile_number // GRID_COLS % GRID_ROWS
    tile_col = tile_number % GRID_COLS
    jitter = jax.random.randint(jax.random.fold_in(key, 7), (TILES, 2), -1, 2)
    anchored = (tile_row == 0) & (tile_col == 0)
    forced = (tile_row == 1) & (tile_col == 1)
    row_jitter = jnp.where(anchored, 0, jnp.where(forced, 1, jitter[:, 0]))
    col_jitter = jnp.where(anchored, 0, jnp.where(forced, 1, jitter[:, 1]))
    center_row = tile_row + row_jitter
    center_col = tile_col + col_jitter
    groups = []
    for frame_step in (-1, 0, 1):
        cand_ids = []
        cand_inside = []
        for row_step in (-1, 0, 1):
            for col_step in (-1, 0, 1):
                near_frame = tile_frame + frame_step
                near_row = center_row + row_step
                near_col = center_col + col_step
                inside_grid = (near_frame >= 0) & (near_frame < GRID_FRAMES) & (near_row >= 0) & (near_row < GRID_ROWS) & (near_col >= 0) & (near_col < GRID_COLS)
                cand_ids.append((near_frame * GRID_ROWS + near_row) * GRID_COLS + near_col)
                cand_inside.append(inside_grid)
        cand_ids = jnp.stack(cand_ids, axis=1)
        cand_inside = jnp.stack(cand_inside, axis=1)
        ranking = jnp.where(cand_inside, 0, 1) * 16 + jnp.arange(9, dtype=jnp.int32)[None, :]
        slot_order = jnp.argsort(ranking, axis=1)[:, :FRAME_SLOTS]
        chosen = jnp.take_along_axis(cand_ids, slot_order, axis=1)
        chosen_inside = jnp.take_along_axis(cand_inside, slot_order, axis=1)
        groups.append(jnp.where(chosen_inside, chosen, -1))
    return jnp.concatenate(groups, axis=1).astype(jnp.int32)


def level_of(own_key, extent, pieces, low, high):
    factor_of, own = 1.0, jax.random.fold_in(own_key, 6)
    for position, parts in pieces:
        heights = jnp.exp(jax.random.uniform(jax.random.fold_in(own, position), (parts,), jnp.float32, low / len(pieces), high / len(pieces)))
        factor_of = factor_of * jnp.repeat(heights, extent[position] // parts).reshape([-1 if axis == position else 1 for axis in range(len(extent))])
    return factor_of


def centred(key, extent, scale, bound, pieces=(), kind=jnp.bfloat16):
    values = jax.random.normal(key, extent, jnp.float32) * scale
    if len(pieces) > 0:
        values = level_of(key, extent, pieces, -0.22, 0.18) * values
    return jnp.clip(values, min=-bound, max=bound).astype(kind)


def setup_inputs(seed: int = 0) -> dict:
    key_of = jax.random.split(jax.random.key(seed), 7)
    return {
        "query_states": draw_query_states(jax.random.fold_in(key_of[6], 71), 0),
        "key_states": draw_key_states(jax.random.fold_in(key_of[6], 71), 0),
        "value_states": centred(key_of[2], (TOKENS, MODEL_DIM), 1.0, 6.0, ((0, 8), (1, 4))),
        "query_gain": jnp.clip(1.0 + 1.5 * jax.random.uniform(key_of[3], (MODEL_DIM,), jnp.float32) ** level_of(key_of[3], (MODEL_DIM,), ((0, 4),), -0.2, 0.2), 1.0, 2.5),
        "key_gain": jnp.clip(1.0 + 1.5 * jax.random.uniform(key_of[4], (MODEL_DIM,), jnp.float32) ** level_of(key_of[4], (MODEL_DIM,), ((0, 4),), -0.2, 0.2), 1.0, 2.5),
        "windows": draw_windows(jax.random.fold_in(key_of[6], 71), 0),
    }


def normalize(source, scale_gain):
    widened = source.astype(jnp.float32)
    mean_square = lax.optimization_barrier(jnp.sum(widened * widened, axis=1, keepdims=True)) / MODEL_DIM
    return (widened * lax.rsqrt(mean_square + 1e-06) * scale_gain).astype(jnp.bfloat16)

def heads_tiles(source):
    return source.reshape(TILES, TILE_TOKENS, HEADS, HEAD_DIM).transpose(2, 0, 1, 3)

def reference(query_states, key_states, value_states, query_gain, key_gain, windows):
    query_normed = normalize(query_states, query_gain)
    key_normed = normalize(key_states, key_gain)
    query_heads = heads_tiles(query_normed)
    key_heads = heads_tiles(key_normed)
    value_heads = heads_tiles(value_states)
    valid_slots = windows >= 0
    safe_ids = jnp.where(valid_slots, windows, 0).astype(jnp.int32)
    score_scale = 1.0 / math.sqrt(HEAD_DIM)

    def one_head(head_arrays):
        query_head, key_head, value_head = head_arrays

        def one_tile(tile_index):
            tile_ids = safe_ids[tile_index]
            key_mask = jnp.repeat(valid_slots[tile_index], TILE_TOKENS)
            key_window = key_head[tile_ids].reshape(WINDOW_SLOTS * TILE_TOKENS, HEAD_DIM)
            value_window = value_head[tile_ids].reshape(WINDOW_SLOTS * TILE_TOKENS, HEAD_DIM)
            scores = jnp.dot(query_head[tile_index], key_window.T, preferred_element_type=jnp.float32) * score_scale
            scores = jnp.where(key_mask[None, :], scores, -jnp.inf)
            row_max = lax.optimization_barrier(jnp.max(scores, axis=1, keepdims=True))
            weights = jnp.exp(scores - row_max)
            weight_sum = lax.optimization_barrier(jnp.sum(weights, axis=1, keepdims=True))
            mixed = jnp.dot(weights.astype(jnp.bfloat16), value_window, preferred_element_type=jnp.float32)
            return (mixed / weight_sum).astype(jnp.bfloat16)
        return lax.map(one_tile, jnp.arange(TILES, dtype=jnp.int32))
    outputs = lax.map(one_head, (query_heads, key_heads, value_heads))
    return outputs.transpose(1, 2, 0, 3).reshape(TOKENS, MODEL_DIM)
```

```python
import math

import jax
import jax.numpy as jnp
from jax import lax
from jax.experimental import pallas as pl
from jax.experimental.pallas import tpu as pltpu
from jax.sharding import PartitionSpec as P

HEAD_DIM = 128
MODEL_DIM = 3072
TILE_TOKENS = 256
WINDOW_SLOTS = 27


def square_sums(source):
    widened = source.astype(jnp.float32)
    return jnp.sum(widened * widened, axis=1)


def normalize_rows(source, totals, scale_gain):
    widened = source.astype(jnp.float32)
    return (widened * lax.rsqrt(totals[:, None] / MODEL_DIM + 1e-06) * scale_gain).astype(
        jnp.bfloat16
    )


def compact_windows(windows, tile_count):
    valid = windows >= 0
    order = jnp.argsort(jnp.logical_not(valid).astype(jnp.int32), axis=1, stable=True)
    ids = jnp.take_along_axis(windows, order, axis=1)
    counts = jnp.sum(valid.astype(jnp.int32), axis=1)
    last = jnp.take_along_axis(ids, jnp.maximum(counts - 1, 0)[:, None], axis=1)
    slot = lax.broadcasted_iota(jnp.int32, ids.shape, 1)
    ids = jnp.where(slot < counts[:, None], ids, last)
    ids = jnp.clip(ids, 0, tile_count - 1)
    return ids.reshape(-1).astype(jnp.int32), counts.astype(jnp.int32)


def attention_kernel(ids_ref, cnt_ref, q_ref, k_ref, v_ref, o_ref, m_sc, l_sc, acc_sc):
    t = pl.program_id(0)
    s = pl.program_id(1)
    heads = q_ref.shape[1] // HEAD_DIM
    score_scale = 1.0 / math.sqrt(HEAD_DIM)

    @pl.when(s == 0)
    def _init():
        m_sc[...] = jnp.full(m_sc.shape, -jnp.inf, jnp.float32)
        l_sc[...] = jnp.zeros(l_sc.shape, jnp.float32)
        acc_sc[...] = jnp.zeros(acc_sc.shape, jnp.float32)

    @pl.when(s < cnt_ref[t])
    def _step():
        for h in range(heads):
            cols = slice(h * HEAD_DIM, (h + 1) * HEAD_DIM)
            q = q_ref[:, cols]
            k = k_ref[0, :, cols]
            v = v_ref[0, :, cols]
            scores = (
                lax.dot_general(
                    q, k, (((1,), (1,)), ((), ())), preferred_element_type=jnp.float32
                )
                * score_scale
            )
            m_prev = m_sc[h]
            m_cur = jnp.max(scores, axis=1, keepdims=True)
            m_new = jnp.maximum(m_prev, m_cur)
            alpha = jnp.exp(m_prev - m_new)
            weights = jnp.exp(scores - m_new[:, :1])
            l_sc[h] = alpha * l_sc[h] + jnp.sum(weights, axis=1, keepdims=True)
            m_sc[h] = m_new
            mixed = jnp.dot(
                weights.astype(jnp.bfloat16), v, preferred_element_type=jnp.float32
            )
            acc_sc[:, cols] = acc_sc[:, cols] * alpha + mixed

    @pl.when(s == pl.num_programs(1) - 1)
    def _finish():
        for h in range(heads):
            cols = slice(h * HEAD_DIM, (h + 1) * HEAD_DIM)
            o_ref[:, cols] = (acc_sc[:, cols] / l_sc[h]).astype(o_ref.dtype)


def window_attention(query_normed, paired, ids, counts):
    rows, width = query_normed.shape
    local_tiles = rows // TILE_TOKENS
    heads = width // HEAD_DIM
    grid_spec = pltpu.PrefetchScalarGridSpec(
        num_scalar_prefetch=2,
        grid=(local_tiles, WINDOW_SLOTS),
        in_specs=[
            pl.BlockSpec((TILE_TOKENS, width), lambda t, s, ids, cnt: (t, 0)),
            pl.BlockSpec(
                (1, TILE_TOKENS, width),
                lambda t, s, ids, cnt: (0, ids[t * WINDOW_SLOTS + s], 0),
            ),
            pl.BlockSpec(
                (1, TILE_TOKENS, width),
                lambda t, s, ids, cnt: (1, ids[t * WINDOW_SLOTS + s], 0),
            ),
        ],
        out_specs=pl.BlockSpec((TILE_TOKENS, width), lambda t, s, ids, cnt: (t, 0)),
        scratch_shapes=[
            pltpu.VMEM((heads, TILE_TOKENS, HEAD_DIM), jnp.float32),
            pltpu.VMEM((heads, TILE_TOKENS, HEAD_DIM), jnp.float32),
            pltpu.VMEM((TILE_TOKENS, width), jnp.float32),
        ],
    )
    return pl.pallas_call(
        attention_kernel,
        grid_spec=grid_spec,
        out_shape=jax.ShapeDtypeStruct((rows, width), jnp.bfloat16),
        compiler_params=pltpu.CompilerParams(
            dimension_semantics=("arbitrary", "arbitrary")
        ),
    )(ids, counts, query_normed, paired, paired)


def on_device(query_states, key_states, value_states, query_gain, key_gain, windows):
    query_total, key_total = lax.psum((square_sums(query_states), square_sums(key_states)), "head")
    query_normed = normalize_rows(query_states, query_total, query_gain)
    sent_keys = normalize_rows(key_states, key_total, key_gain)
    paired = jnp.stack([sent_keys, value_states])
    extended = lax.all_gather(paired, "tok", axis=1, tiled=True)
    tile_count = extended.shape[1] // TILE_TOKENS
    ids, counts = compact_windows(windows, tile_count)
    return window_attention(query_normed, extended, ids, counts)


def solution(mesh):
    in_specs = (
        P("tok", "head"),
        P("tok", "head"),
        P("tok", "head"),
        P("head"),
        P("head"),
        P("tok", None),
    )
    out_specs = P("tok", "head")
    return jax.shard_map(
        on_device, mesh=mesh, in_specs=in_specs, out_specs=out_specs, check_vma=False
    )
```

```python
import math

import jax
import jax.numpy as jnp
from jax import lax
from jax.experimental import pallas as pl
from jax.experimental.pallas import tpu as pltpu
from jax.sharding import PartitionSpec as P

HEAD_DIM = 128
MODEL_DIM = 3072
TILE_TOKENS = 256
WINDOW_SLOTS = 27


def square_sums(source):
    widened = source.astype(jnp.float32)
    return jnp.sum(widened * widened, axis=1)


def normalize_rows(source, totals, scale_gain):
    widened = source.astype(jnp.float32)
    return (widened * lax.rsqrt(totals[:, None] / MODEL_DIM + 1e-06) * scale_gain).astype(
        jnp.bfloat16
    )


def compact_windows(windows, tile_count):
    valid = windows >= 0
    order = jnp.argsort(jnp.logical_not(valid).astype(jnp.int32), axis=1, stable=True)
    ids = jnp.take_along_axis(windows, order, axis=1)
    counts = jnp.sum(valid.astype(jnp.int32), axis=1)
    last = jnp.take_along_axis(ids, jnp.maximum(counts - 1, 0)[:, None], axis=1)
    slot = lax.broadcasted_iota(jnp.int32, ids.shape, 1)
    ids = jnp.where(slot < counts[:, None], ids, last)
    ids = jnp.clip(ids, 0, tile_count - 1)
    return ids.reshape(-1).astype(jnp.int32), counts.astype(jnp.int32)


def attention_kernel(ids_ref, cnt_ref, q_ref, k_ref, v_ref, o_ref, m_sc, l_sc, acc_sc):
    t = pl.program_id(0)
    s = pl.program_id(1)
    heads = q_ref.shape[1] // HEAD_DIM
    score_scale = 1.0 / math.sqrt(HEAD_DIM)

    @pl.when(s == 0)
    def _init():
        m_sc[...] = jnp.full(m_sc.shape, -jnp.inf, jnp.float32)
        l_sc[...] = jnp.zeros(l_sc.shape, jnp.float32)
        acc_sc[...] = jnp.zeros(acc_sc.shape, jnp.float32)

    @pl.when(s < cnt_ref[t])
    def _step():
        for h in range(heads):
            cols = slice(h * HEAD_DIM, (h + 1) * HEAD_DIM)
            q = q_ref[:, cols]
            k = k_ref[0, :, cols]
            v = v_ref[0, :, cols]
            scores = (
                lax.dot_general(
                    q, k, (((1,), (1,)), ((), ())), preferred_element_type=jnp.float32
                )
                * score_scale
            )
            m_prev = m_sc[h]
            m_cur = jnp.max(scores, axis=1, keepdims=True)
            m_new = jnp.maximum(m_prev, m_cur)
            alpha = jnp.exp(m_prev - m_new)
            weights = jnp.exp(scores - m_new[:, :1])
            l_sc[h] = alpha * l_sc[h] + jnp.sum(weights, axis=1, keepdims=True)
            m_sc[h] = m_new
            mixed = jnp.dot(
                weights.astype(jnp.bfloat16), v, preferred_element_type=jnp.float32
            )
            acc_sc[:, cols] = acc_sc[:, cols] * alpha + mixed

    @pl.when(s == pl.num_programs(1) - 1)
    def _finish():
        for h in range(heads):
            cols = slice(h * HEAD_DIM, (h + 1) * HEAD_DIM)
            o_ref[:, cols] = (acc_sc[:, cols] / l_sc[h]).astype(o_ref.dtype)


def window_attention(query_normed, keys, key_lead, values, value_lead, ids, counts, group, groups, previous):
    rows, width = query_normed.shape
    local_tiles = rows // TILE_TOKENS
    group_width = width // groups
    heads = group_width // HEAD_DIM
    in_specs = [
        pl.BlockSpec((TILE_TOKENS, group_width), lambda t, s, ids, cnt: (t, group)),
        pl.BlockSpec(
            (1, TILE_TOKENS, group_width),
            lambda t, s, ids, cnt: (key_lead, ids[t * WINDOW_SLOTS + s], 0),
        ),
        pl.BlockSpec(
            (1, TILE_TOKENS, group_width),
            lambda t, s, ids, cnt: (value_lead, ids[t * WINDOW_SLOTS + s], 0),
        ),
    ]
    operands = [ids, counts, query_normed, keys, values]
    aliases = {}
    kernel = attention_kernel
    if previous is not None:
        in_specs.append(pl.BlockSpec(memory_space=pl.ANY))
        operands.append(previous)
        aliases = {5: 0}

        def kernel(ids_ref, cnt_ref, q_ref, k_ref, v_ref, prev_ref, o_ref, m_sc, l_sc, acc_sc):
            attention_kernel(ids_ref, cnt_ref, q_ref, k_ref, v_ref, o_ref, m_sc, l_sc, acc_sc)

    grid_spec = pltpu.PrefetchScalarGridSpec(
        num_scalar_prefetch=2,
        grid=(local_tiles, WINDOW_SLOTS),
        in_specs=in_specs,
        out_specs=pl.BlockSpec((TILE_TOKENS, group_width), lambda t, s, ids, cnt: (t, group)),
        scratch_shapes=[
            pltpu.VMEM((heads, TILE_TOKENS, HEAD_DIM), jnp.float32),
            pltpu.VMEM((heads, TILE_TOKENS, HEAD_DIM), jnp.float32),
            pltpu.VMEM((TILE_TOKENS, group_width), jnp.float32),
        ],
    )
    return pl.pallas_call(
        kernel,
        grid_spec=grid_spec,
        out_shape=jax.ShapeDtypeStruct((rows, width), jnp.bfloat16),
        input_output_aliases=aliases,
        compiler_params=pltpu.CompilerParams(
            dimension_semantics=("arbitrary", "arbitrary")
        ),
    )(*operands)


def on_device(query_states, key_states, value_states, query_gain, key_gain, windows):
    width = query_states.shape[1]
    heads_here = width // HEAD_DIM
    groups = 3 if heads_here % 3 == 0 else 1
    group_width = width // groups

    def columns(source, group):
        return source[:, group * group_width:(group + 1) * group_width]

    first_values = lax.all_gather(columns(value_states, 0), "tok", axis=0, tiled=True)
    query_total, key_total = lax.psum((square_sums(query_states), square_sums(key_states)), "head")
    query_normed = normalize_rows(query_states, query_total, query_gain)
    sent_keys = normalize_rows(key_states, key_total, key_gain)
    first_keys = lax.all_gather(columns(sent_keys, 0), "tok", axis=0, tiled=True)
    tile_count = first_keys.shape[0] // TILE_TOKENS
    ids, counts = compact_windows(windows, tile_count)
    output = window_attention(
        query_normed, first_keys[None], 0, first_values[None], 0, ids, counts, 0, groups, None
    )
    for group in range(1, groups):
        paired = jnp.stack([columns(sent_keys, group), columns(value_states, group)])
        extended = lax.all_gather(paired, "tok", axis=1, tiled=True)
        output = window_attention(
            query_normed, extended, 0, extended, 1, ids, counts, group, groups, output
        )
    return output


def solution(mesh):
    in_specs = (
        P("tok", "head"),
        P("tok", "head"),
        P("tok", "head"),
        P("head"),
        P("head"),
        P("tok", None),
    )
    out_specs = P("tok", "head")
    return jax.shard_map(
        on_device, mesh=mesh, in_specs=in_specs, out_specs=out_specs, check_vma=False
    )
```

```python
import functools
import math

import jax
import jax.numpy as jnp
from jax import lax
from jax.experimental import pallas as pl
from jax.experimental.pallas import tpu as pltpu
from jax.sharding import PartitionSpec as P

HEAD_DIM = 128
MODEL_DIM = 3072
TILE_TOKENS = 256
WINDOW_SLOTS = 27
FRAME_ROWS = 4
FRAME_COLS = 4


def square_sums(source):
    widened = source.astype(jnp.float32)
    return jnp.sum(widened * widened, axis=1)


def normalize_rows(source, totals, scale_gain):
    widened = source.astype(jnp.float32)
    return (widened * lax.rsqrt(totals[:, None] / MODEL_DIM + 1e-06) * scale_gain).astype(
        jnp.bfloat16
    )


def compact_windows(windows, tile_count):
    valid = windows >= 0
    order = jnp.argsort(jnp.logical_not(valid).astype(jnp.int32), axis=1, stable=True)
    ids = jnp.take_along_axis(windows, order, axis=1)
    counts = jnp.sum(valid.astype(jnp.int32), axis=1)
    last = jnp.take_along_axis(ids, jnp.maximum(counts - 1, 0)[:, None], axis=1)
    slot = lax.broadcasted_iota(jnp.int32, ids.shape, 1)
    ids = jnp.where(slot < counts[:, None], ids, last)
    ids = jnp.clip(ids, 0, tile_count - 1)
    return ids.reshape(-1).astype(jnp.int32), counts.astype(jnp.int32)


def attention_kernel(ids_ref, cnt_ref, q_ref, k_ref, v_ref, o_ref, m_sc, l_sc, acc_sc):
    t = pl.program_id(0)
    s = pl.program_id(1)
    heads = q_ref.shape[1] // HEAD_DIM
    score_scale = 1.0 / math.sqrt(HEAD_DIM)

    @pl.when(s == 0)
    def _init():
        m_sc[...] = jnp.full(m_sc.shape, -jnp.inf, jnp.float32)
        l_sc[...] = jnp.zeros(l_sc.shape, jnp.float32)
        acc_sc[...] = jnp.zeros(acc_sc.shape, jnp.float32)

    @pl.when(s < cnt_ref[t])
    def _step():
        for h in range(heads):
            cols = slice(h * HEAD_DIM, (h + 1) * HEAD_DIM)
            q = q_ref[:, cols]
            k = k_ref[0, :, cols]
            v = v_ref[0, :, cols]
            scores = (
                lax.dot_general(
                    q, k, (((1,), (1,)), ((), ())), preferred_element_type=jnp.float32
                )
                * score_scale
            )
            m_prev = m_sc[h]
            m_cur = jnp.max(scores, axis=1, keepdims=True)
            m_new = jnp.maximum(m_prev, m_cur)
            alpha = jnp.exp(m_prev - m_new)
            weights = jnp.exp(scores - m_new[:, :1])
            l_sc[h] = alpha * l_sc[h] + jnp.sum(weights, axis=1, keepdims=True)
            m_sc[h] = m_new
            mixed = jnp.dot(
                weights.astype(jnp.bfloat16), v, preferred_element_type=jnp.float32
            )
            acc_sc[:, cols] = acc_sc[:, cols] * alpha + mixed

    @pl.when(s == pl.num_programs(1) - 1)
    def _finish():
        for h in range(heads):
            cols = slice(h * HEAD_DIM, (h + 1) * HEAD_DIM)
            o_ref[:, cols] = (acc_sc[:, cols] / l_sc[h]).astype(o_ref.dtype)


def window_attention(query_normed, keys, key_lead, values, value_lead, ids, counts, group, groups, previous):
    rows, width = query_normed.shape
    local_tiles = rows // TILE_TOKENS
    group_width = width // groups
    heads = group_width // HEAD_DIM
    in_specs = [
        pl.BlockSpec((TILE_TOKENS, group_width), lambda t, s, ids, cnt: (t, group)),
        pl.BlockSpec(
            (1, TILE_TOKENS, group_width),
            lambda t, s, ids, cnt: (key_lead, ids[t * WINDOW_SLOTS + s], 0),
        ),
        pl.BlockSpec(
            (1, TILE_TOKENS, group_width),
            lambda t, s, ids, cnt: (value_lead, ids[t * WINDOW_SLOTS + s], 0),
        ),
    ]
    operands = [ids, counts, query_normed, keys, values]
    aliases = {}
    kernel = attention_kernel
    if previous is not None:
        in_specs.append(pl.BlockSpec(memory_space=pl.ANY))
        operands.append(previous)
        aliases = {5: 0}

        def kernel(ids_ref, cnt_ref, q_ref, k_ref, v_ref, prev_ref, o_ref, m_sc, l_sc, acc_sc):
            attention_kernel(ids_ref, cnt_ref, q_ref, k_ref, v_ref, o_ref, m_sc, l_sc, acc_sc)

    grid_spec = pltpu.PrefetchScalarGridSpec(
        num_scalar_prefetch=2,
        grid=(local_tiles, WINDOW_SLOTS),
        in_specs=in_specs,
        out_specs=pl.BlockSpec((TILE_TOKENS, group_width), lambda t, s, ids, cnt: (t, group)),
        scratch_shapes=[
            pltpu.VMEM((heads, TILE_TOKENS, HEAD_DIM), jnp.float32),
            pltpu.VMEM((heads, TILE_TOKENS, HEAD_DIM), jnp.float32),
            pltpu.VMEM((TILE_TOKENS, group_width), jnp.float32),
        ],
    )
    return pl.pallas_call(
        kernel,
        grid_spec=grid_spec,
        out_shape=jax.ShapeDtypeStruct((rows, width), jnp.bfloat16),
        input_output_aliases=aliases,
        cost_estimate=pl.CostEstimate(
            flops=4 * rows * WINDOW_SLOTS * TILE_TOKENS * group_width,
            transcendentals=rows * WINDOW_SLOTS * TILE_TOKENS * heads,
            bytes_accessed=4 * rows * WINDOW_SLOTS * group_width,
        ),
        compiler_params=pltpu.CompilerParams(
            dimension_semantics=("arbitrary", "arbitrary")
        ),
    )(*operands)


def needed_span(chip, local_tiles, tile_count):
    per_frame = FRAME_ROWS * FRAME_COLS
    lowest, highest = tile_count, -1
    for i in range(2 * chip * local_tiles, (2 * chip + 2) * local_tiles):
        fi, ri, ci = i // per_frame, i // FRAME_COLS % FRAME_ROWS, i % FRAME_COLS
        for j in range(tile_count):
            fj, rj, cj = j // per_frame, j // FRAME_COLS % FRAME_ROWS, j % FRAME_COLS
            if abs(fi - fj) <= 1 and abs(ri - rj) <= 2 and abs(ci - cj) <= 2:
                lowest = min(lowest, j)
                highest = max(highest, j)
    return lowest // local_tiles, highest // local_tiles


def chain(block, direction, steps, spans, chips):
    received = []
    current = block
    for step in range(1, steps + 1):
        pairs = []
        for chip in range(chips):
            sender = chip - direction
            origin = chip - direction * step
            if not (0 <= sender < chips and 0 <= origin < chips):
                continue
            for core in range(2):
                shard = 2 * origin + core
                beyond = range(chip, chips) if direction > 0 else range(0, chip + 1)
                if any(
                    spans[other][0] <= shard <= spans[other][1]
                    and abs(other - origin) <= steps
                    for other in beyond
                ):
                    pairs.append((2 * sender + core, 2 * chip + core))
        if pairs:
            current = lax.ppermute(current, "tok", pairs)
        else:
            current = jnp.zeros_like(current)
        received.append(current)
    return received


def on_device(query_states, key_states, value_states, query_gain, key_gain, windows, tok_count):
    rows, width = query_states.shape
    local_tiles = rows // TILE_TOKENS
    tile_count = tok_count * local_tiles
    chips = tok_count // 2
    spans = [needed_span(chip, local_tiles, tile_count) for chip in range(chips)]
    behind = max(chip - spans[chip][0] // 2 for chip in range(chips))
    ahead = max(spans[chip][1] // 2 - chip for chip in range(chips))
    heads_here = width // HEAD_DIM
    groups = 3 if heads_here % 3 == 0 else 1
    group_width = width // groups

    def columns(source, group):
        return source[:, group * group_width:(group + 1) * group_width]

    query_total, key_total = lax.psum((square_sums(query_states), square_sums(key_states)), "head")
    query_normed = normalize_rows(query_states, query_total, query_gain)
    sent_keys = normalize_rows(key_states, key_total, key_gain)

    position = lax.axis_index("tok")
    core = position % 2
    chip = position // 2
    window_tiles = 2 * (behind + ahead + 1) * local_tiles
    base_tile = 2 * (chip - behind) * local_tiles
    ids, counts = compact_windows(windows, tile_count)
    ids = jnp.clip(ids - base_tile, 0, window_tiles - 1)
    partner_pairs = [(t, t ^ 1) for t in range(tok_count)]

    def exchange(mine):
        partner = lax.ppermute(mine, "tok", partner_pairs)
        first = jnp.where(core == 0, mine, partner)
        second = jnp.where(core == 0, partner, mine)
        buffer = jnp.stack([first, second], axis=1).transpose(2, 0, 1, 3, 4)
        return buffer.reshape(2, window_tiles * TILE_TOKENS, group_width)

    def gather_group(group, keys, values):
        block = jnp.stack([columns(keys, group), columns(values, group)])
        from_behind = chain(block, 1, behind, spans, chips)
        from_ahead = chain(block, -1, ahead, spans, chips)
        return jnp.stack(from_behind[::-1] + [block] + from_ahead)

    keys, values = sent_keys, value_states
    buffer = exchange(gather_group(0, keys, values))
    output = None
    for group in range(groups):
        if group + 1 < groups:
            buffer, keys, values = lax.optimization_barrier((buffer, keys, values))
            mine = gather_group(group + 1, keys, values)
        output = window_attention(
            query_normed, buffer, 0, buffer, 1, ids, counts, group, groups, output
        )
        if group + 1 < groups:
            output, mine = lax.optimization_barrier((output, mine))
            buffer = exchange(mine)
    return output


def solution(mesh):
    in_specs = (
        P("tok", "head"),
        P("tok", "head"),
        P("tok", "head"),
        P("head"),
        P("head"),
        P("tok", None),
    )
    out_specs = P("tok", "head")
    return jax.shard_map(
        functools.partial(on_device, tok_count=mesh.shape["tok"]),
        mesh=mesh,
        in_specs=in_specs,
        out_specs=out_specs,
        check_vma=False,
    )
```

```python
import math

import jax
import jax.numpy as jnp
from jax import lax
from jax.experimental import pallas as pl
from jax.experimental.pallas import tpu as pltpu
from jax.sharding import PartitionSpec as P

HEAD_DIM = 128
MODEL_DIM = 3072
TILE_TOKENS = 256
WINDOW_SLOTS = 27


def square_sums(source):
    widened = source.astype(jnp.float32)
    return jnp.sum(widened * widened, axis=1)


def normalize_rows(source, totals, scale_gain):
    widened = source.astype(jnp.float32)
    return (widened * lax.rsqrt(totals[:, None] / MODEL_DIM + 1e-06) * scale_gain).astype(
        jnp.bfloat16
    )


def compact_windows(windows, tile_count):
    valid = windows >= 0
    order = jnp.argsort(jnp.logical_not(valid).astype(jnp.int32), axis=1, stable=True)
    ids = jnp.take_along_axis(windows, order, axis=1)
    counts = jnp.sum(valid.astype(jnp.int32), axis=1)
    last = jnp.take_along_axis(ids, jnp.maximum(counts - 1, 0)[:, None], axis=1)
    slot = lax.broadcasted_iota(jnp.int32, ids.shape, 1)
    ids = jnp.where(slot < counts[:, None], ids, last)
    ids = jnp.clip(ids, 0, tile_count - 1)
    return ids.reshape(-1).astype(jnp.int32), counts.astype(jnp.int32)


def attention_kernel(ids_ref, cnt_ref, q_ref, k_ref, v_ref, o_ref, m_sc, l_sc, acc_sc):
    t = pl.program_id(0)
    s = pl.program_id(1)
    heads = q_ref.shape[1] // HEAD_DIM
    score_scale = 1.0 / math.sqrt(HEAD_DIM)

    @pl.when(s == 0)
    def _init():
        m_sc[...] = jnp.full(m_sc.shape, -jnp.inf, jnp.float32)
        l_sc[...] = jnp.zeros(l_sc.shape, jnp.float32)
        acc_sc[...] = jnp.zeros(acc_sc.shape, jnp.float32)

    @pl.when(s < cnt_ref[t])
    def _step():
        for h in range(heads):
            cols = slice(h * HEAD_DIM, (h + 1) * HEAD_DIM)
            q = q_ref[:, cols]
            k = k_ref[0, :, cols]
            v = v_ref[0, :, cols]
            scores = (
                lax.dot_general(
                    q, k, (((1,), (1,)), ((), ())), preferred_element_type=jnp.float32
                )
                * score_scale
            )
            m_prev = m_sc[h]
            m_cur = jnp.max(scores, axis=1, keepdims=True)
            m_new = jnp.maximum(m_prev, m_cur)
            alpha = jnp.exp(m_prev - m_new)
            weights = jnp.exp(scores - m_new[:, :1])
            l_sc[h] = alpha * l_sc[h] + jnp.sum(weights, axis=1, keepdims=True)
            m_sc[h] = m_new
            mixed = jnp.dot(
                weights.astype(jnp.bfloat16), v, preferred_element_type=jnp.float32
            )
            acc_sc[:, cols] = acc_sc[:, cols] * alpha + mixed

    @pl.when(s == pl.num_programs(1) - 1)
    def _finish():
        for h in range(heads):
            cols = slice(h * HEAD_DIM, (h + 1) * HEAD_DIM)
            o_ref[:, cols] = (acc_sc[:, cols] / l_sc[h]).astype(o_ref.dtype)


def window_attention(query_normed, keys, key_lead, values, value_lead, ids, counts, offset, group_width, previous):
    rows, width = query_normed.shape
    local_tiles = rows // TILE_TOKENS
    heads = group_width // HEAD_DIM
    group = offset // group_width
    in_specs = [
        pl.BlockSpec((TILE_TOKENS, group_width), lambda t, s, ids, cnt: (t, group)),
        pl.BlockSpec(
            (1, TILE_TOKENS, group_width),
            lambda t, s, ids, cnt: (key_lead, ids[t * WINDOW_SLOTS + s], 0),
        ),
        pl.BlockSpec(
            (1, TILE_TOKENS, group_width),
            lambda t, s, ids, cnt: (value_lead, ids[t * WINDOW_SLOTS + s], 0),
        ),
    ]
    operands = [ids, counts, query_normed, keys, values]
    aliases = {}
    kernel = attention_kernel
    if previous is not None:
        in_specs.append(pl.BlockSpec(memory_space=pl.ANY))
        operands.append(previous)
        aliases = {5: 0}

        def kernel(ids_ref, cnt_ref, q_ref, k_ref, v_ref, prev_ref, o_ref, m_sc, l_sc, acc_sc):
            attention_kernel(ids_ref, cnt_ref, q_ref, k_ref, v_ref, o_ref, m_sc, l_sc, acc_sc)

    grid_spec = pltpu.PrefetchScalarGridSpec(
        num_scalar_prefetch=2,
        grid=(local_tiles, WINDOW_SLOTS),
        in_specs=in_specs,
        out_specs=pl.BlockSpec((TILE_TOKENS, group_width), lambda t, s, ids, cnt: (t, group)),
        scratch_shapes=[
            pltpu.VMEM((heads, TILE_TOKENS, HEAD_DIM), jnp.float32),
            pltpu.VMEM((heads, TILE_TOKENS, HEAD_DIM), jnp.float32),
            pltpu.VMEM((TILE_TOKENS, group_width), jnp.float32),
        ],
    )
    return pl.pallas_call(
        kernel,
        grid_spec=grid_spec,
        out_shape=jax.ShapeDtypeStruct((rows, width), jnp.bfloat16),
        input_output_aliases=aliases,
        compiler_params=pltpu.CompilerParams(
            dimension_semantics=("arbitrary", "arbitrary")
        ),
    )(*operands)


def head_groups(heads_here):
    if heads_here % 2 == 0 and heads_here >= 4:
        return [2] * (heads_here // 2 - 1) + [1, 1]
    return [1] * heads_here


def on_device(query_states, key_states, value_states, query_gain, key_gain, windows):
    sizes = head_groups(query_states.shape[1] // HEAD_DIM)
    offsets = [HEAD_DIM * sum(sizes[:number]) for number in range(len(sizes))]
    widths = [HEAD_DIM * size for size in sizes]

    def columns(source, number):
        return source[:, offsets[number]:offsets[number] + widths[number]]

    query_total, key_total = lax.psum((square_sums(query_states), square_sums(key_states)), "head")
    query_normed = normalize_rows(query_states, query_total, query_gain)
    sent_keys = normalize_rows(key_states, key_total, key_gain)
    tile_count = query_states.shape[0] * lax.psum(1, "tok") // TILE_TOKENS
    ids, counts = compact_windows(windows, tile_count)
    output = None
    for number in range(len(sizes)):
        paired = jnp.stack([columns(sent_keys, number), columns(value_states, number)])
        extended = lax.all_gather(paired, "tok", axis=1, tiled=True)
        output = window_attention(
            query_normed, extended, 0, extended, 1, ids, counts,
            offsets[number], widths[number], output,
        )
    return output


def solution(mesh):
    in_specs = (
        P("tok", "head"),
        P("tok", "head"),
        P("tok", "head"),
        P("head"),
        P("head"),
        P("tok", None),
    )
    out_specs = P("tok", "head")
    return jax.shard_map(
        on_device, mesh=mesh, in_specs=in_specs, out_specs=out_specs, check_vma=False
    )
```

```python
import math

import jax
import jax.numpy as jnp
from jax import lax
from jax.experimental import pallas as pl
from jax.experimental.pallas import tpu as pltpu
from jax.sharding import PartitionSpec as P

HEAD_DIM = 128
MODEL_DIM = 3072
TILE_TOKENS = 256
WINDOW_SLOTS = 27
SLOTS_PER_STEP = 3


def square_sums(source):
    widened = source.astype(jnp.float32)
    return jnp.sum(widened * widened, axis=1)


def normalize_rows(source, totals, scale_gain):
    widened = source.astype(jnp.float32)
    return (widened * lax.rsqrt(totals[:, None] / MODEL_DIM + 1e-06) * scale_gain).astype(
        jnp.bfloat16
    )


def compact_windows(windows, tile_count):
    valid = windows >= 0
    order = jnp.argsort(jnp.logical_not(valid).astype(jnp.int32), axis=1, stable=True)
    ids = jnp.take_along_axis(windows, order, axis=1)
    counts = jnp.sum(valid.astype(jnp.int32), axis=1)
    last = jnp.take_along_axis(ids, jnp.maximum(counts - 1, 0)[:, None], axis=1)
    slot = lax.broadcasted_iota(jnp.int32, ids.shape, 1)
    ids = jnp.where(slot < counts[:, None], ids, last)
    ids = jnp.clip(ids, 0, tile_count - 1)
    return ids.reshape(-1).astype(jnp.int32), counts.astype(jnp.int32)


def attention_kernel(ids_ref, cnt_ref, q_ref, *refs):
    k_refs = refs[:SLOTS_PER_STEP]
    v_refs = refs[SLOTS_PER_STEP:2 * SLOTS_PER_STEP]
    o_ref, m_sc, l_sc, acc_sc = refs[-4:]
    t = pl.program_id(0)
    j = pl.program_id(1)
    heads = q_ref.shape[1] // HEAD_DIM
    score_scale = 1.0 / math.sqrt(HEAD_DIM)

    @pl.when(j == 0)
    def _init():
        m_sc[...] = jnp.full(m_sc.shape, -jnp.inf, jnp.float32)
        l_sc[...] = jnp.zeros(l_sc.shape, jnp.float32)
        acc_sc[...] = jnp.zeros(acc_sc.shape, jnp.float32)

    for sub in range(SLOTS_PER_STEP):
        k_ref = k_refs[sub]
        v_ref = v_refs[sub]

        @pl.when(j * SLOTS_PER_STEP + sub < cnt_ref[t])
        def _step():
            for h in range(heads):
                cols = slice(h * HEAD_DIM, (h + 1) * HEAD_DIM)
                q = q_ref[:, cols]
                k = k_ref[0, :, cols]
                v = v_ref[0, :, cols]
                scores = (
                    lax.dot_general(
                        q, k, (((1,), (1,)), ((), ())), preferred_element_type=jnp.float32
                    )
                    * score_scale
                )
                m_prev = m_sc[h]
                m_cur = jnp.max(scores, axis=1, keepdims=True)
                m_new = jnp.maximum(m_prev, m_cur)
                alpha = jnp.exp(m_prev - m_new)
                weights = jnp.exp(scores - m_new[:, :1])
                l_sc[h] = alpha * l_sc[h] + jnp.sum(weights, axis=1, keepdims=True)
                m_sc[h] = m_new
                mixed = jnp.dot(
                    weights.astype(jnp.bfloat16), v, preferred_element_type=jnp.float32
                )
                acc_sc[:, cols] = acc_sc[:, cols] * alpha + mixed

    @pl.when(j == pl.num_programs(1) - 1)
    def _finish():
        for h in range(heads):
            cols = slice(h * HEAD_DIM, (h + 1) * HEAD_DIM)
            o_ref[:, cols] = (acc_sc[:, cols] / l_sc[h]).astype(o_ref.dtype)


def window_attention(query_normed, keys, key_lead, values, value_lead, ids, counts, offset, group_width, previous):
    rows, width = query_normed.shape
    local_tiles = rows // TILE_TOKENS
    heads = group_width // HEAD_DIM
    group = offset // group_width
    steps = WINDOW_SLOTS // SLOTS_PER_STEP

    def window_spec(lead, sub):
        return pl.BlockSpec(
            (1, TILE_TOKENS, group_width),
            lambda t, j, ids, cnt: (lead, ids[t * WINDOW_SLOTS + j * SLOTS_PER_STEP + sub], 0),
        )

    in_specs = [pl.BlockSpec((TILE_TOKENS, group_width), lambda t, j, ids, cnt: (t, group))]
    in_specs += [window_spec(key_lead, sub) for sub in range(SLOTS_PER_STEP)]
    in_specs += [window_spec(value_lead, sub) for sub in range(SLOTS_PER_STEP)]
    operands = [ids, counts, query_normed]
    operands += [keys] * SLOTS_PER_STEP + [values] * SLOTS_PER_STEP
    aliases = {}
    kernel = attention_kernel
    if previous is not None:
        in_specs.append(pl.BlockSpec(memory_space=pl.ANY))
        aliases = {len(operands): 0}
        operands.append(previous)

        def kernel(ids_ref, cnt_ref, q_ref, *refs):
            attention_kernel(ids_ref, cnt_ref, q_ref, *refs[:2 * SLOTS_PER_STEP], *refs[-4:])

    grid_spec = pltpu.PrefetchScalarGridSpec(
        num_scalar_prefetch=2,
        grid=(local_tiles, steps),
        in_specs=in_specs,
        out_specs=pl.BlockSpec((TILE_TOKENS, group_width), lambda t, j, ids, cnt: (t, group)),
        scratch_shapes=[
            pltpu.VMEM((heads, TILE_TOKENS, HEAD_DIM), jnp.float32),
            pltpu.VMEM((heads, TILE_TOKENS, HEAD_DIM), jnp.float32),
            pltpu.VMEM((TILE_TOKENS, group_width), jnp.float32),
        ],
    )
    return pl.pallas_call(
        kernel,
        grid_spec=grid_spec,
        out_shape=jax.ShapeDtypeStruct((rows, width), jnp.bfloat16),
        input_output_aliases=aliases,
        compiler_params=pltpu.CompilerParams(
            dimension_semantics=("arbitrary", "arbitrary")
        ),
    )(*operands)


def head_groups(heads_here):
    if heads_here % 2 == 0 and heads_here >= 4:
        return [2] * (heads_here // 2 - 1) + [1, 1]
    return [1] * heads_here


def on_device(query_states, key_states, value_states, query_gain, key_gain, windows):
    sizes = head_groups(query_states.shape[1] // HEAD_DIM)
    offsets = [HEAD_DIM * sum(sizes[:number]) for number in range(len(sizes))]
    widths = [HEAD_DIM * size for size in sizes]

    def columns(source, number):
        return source[:, offsets[number]:offsets[number] + widths[number]]

    query_total, key_total = lax.psum((square_sums(query_states), square_sums(key_states)), "head")
    query_normed = normalize_rows(query_states, query_total, query_gain)
    sent_keys = normalize_rows(key_states, key_total, key_gain)
    tile_count = query_states.shape[0] * lax.psum(1, "tok") // TILE_TOKENS
    ids, counts = compact_windows(windows, tile_count)
    output = None
    for number in range(len(sizes)):
        paired = jnp.stack([columns(sent_keys, number), columns(value_states, number)])
        extended = lax.all_gather(paired, "tok", axis=1, tiled=True)
        output = window_attention(
            query_normed, extended, 0, extended, 1, ids, counts,
            offsets[number], widths[number], output,
        )
    return output


def solution(mesh):
    in_specs = (
        P("tok", "head"),
        P("tok", "head"),
        P("tok", "head"),
        P("head"),
        P("head"),
        P("tok", None),
    )
    out_specs = P("tok", "head")
    return jax.shard_map(
        on_device, mesh=mesh, in_specs=in_specs, out_specs=out_specs, check_vma=False
    )
```

```python
import functools
import math

import jax
import jax.numpy as jnp
from jax import lax
from jax.experimental import pallas as pl
from jax.experimental.pallas import tpu as pltpu
from jax.sharding import PartitionSpec as P

HEAD_DIM = 128
MODEL_DIM = 3072
TILE_TOKENS = 256
WINDOW_SLOTS = 27
SLOTS_PER_STEP = 3
STATS_HALF = 64


def square_sums(source):
    widened = source.astype(jnp.float32)
    return jnp.sum(widened * widened, axis=1)


def normalize_rows(source, totals, scale_gain):
    widened = source.astype(jnp.float32)
    return (widened * lax.rsqrt(totals[:, None] / MODEL_DIM + 1e-06) * scale_gain).astype(
        jnp.bfloat16
    )


def compact_windows(windows, tile_count):
    valid = windows >= 0
    order = jnp.argsort(jnp.logical_not(valid).astype(jnp.int32), axis=1, stable=True)
    ids = jnp.take_along_axis(windows, order, axis=1)
    counts = jnp.sum(valid.astype(jnp.int32), axis=1)
    last = jnp.take_along_axis(ids, jnp.maximum(counts - 1, 0)[:, None], axis=1)
    slot = lax.broadcasted_iota(jnp.int32, ids.shape, 1)
    ids = jnp.where(slot < counts[:, None], ids, last)
    ids = jnp.clip(ids, 0, tile_count - 1)
    return ids.reshape(-1).astype(jnp.int32), counts.astype(jnp.int32)


def attention_kernel(ids_ref, cnt_ref, q_ref, *refs, first, last):
    k_refs = refs[:SLOTS_PER_STEP]
    v_refs = refs[SLOTS_PER_STEP:2 * SLOTS_PER_STEP]
    rest = refs[2 * SLOTS_PER_STEP:]
    if not first:
        acc_in, stats_in = rest[:2]
        rest = rest[2:]
    if last:
        o_ref = rest[0]
        rest = rest[1:]
    else:
        acc_out, stats_out = rest[:2]
        rest = rest[2:]
    m_sc, l_sc, acc_sc = rest
    t = pl.program_id(0)
    j = pl.program_id(1)
    heads = q_ref.shape[1] // HEAD_DIM
    score_scale = 1.0 / math.sqrt(HEAD_DIM)

    @pl.when(j == 0)
    def _init():
        if first:
            m_sc[...] = jnp.full(m_sc.shape, -jnp.inf, jnp.float32)
            l_sc[...] = jnp.zeros(l_sc.shape, jnp.float32)
            acc_sc[...] = jnp.zeros(acc_sc.shape, jnp.float32)
        else:
            for h in range(heads):
                m_sc[h] = jnp.broadcast_to(stats_in[:, h:h + 1], m_sc.shape[1:])
                l_sc[h] = jnp.broadcast_to(
                    stats_in[:, STATS_HALF + h:STATS_HALF + h + 1], l_sc.shape[1:]
                )
            acc_sc[...] = acc_in[...]

    for sub in range(SLOTS_PER_STEP):
        k_ref = k_refs[sub]
        v_ref = v_refs[sub]

        @pl.when(j * SLOTS_PER_STEP + sub < cnt_ref[t])
        def _step():
            for h in range(heads):
                cols = slice(h * HEAD_DIM, (h + 1) * HEAD_DIM)
                q = q_ref[:, cols]
                k = k_ref[0, :, cols]
                v = v_ref[0, :, cols]
                scores = (
                    lax.dot_general(
                        q, k, (((1,), (1,)), ((), ())), preferred_element_type=jnp.float32
                    )
                    * score_scale
                )
                m_prev = m_sc[h]
                m_cur = jnp.max(scores, axis=1, keepdims=True)
                m_new = jnp.maximum(m_prev, m_cur)
                alpha = jnp.exp(m_prev - m_new)
                weights = jnp.exp(scores - m_new[:, :1])
                l_sc[h] = alpha * l_sc[h] + jnp.sum(weights, axis=1, keepdims=True)
                m_sc[h] = m_new
                mixed = jnp.dot(
                    weights.astype(jnp.bfloat16), v, preferred_element_type=jnp.float32
                )
                acc_sc[:, cols] = acc_sc[:, cols] * alpha + mixed

    @pl.when(j == pl.num_programs(1) - 1)
    def _finish():
        if last:
            for h in range(heads):
                cols = slice(h * HEAD_DIM, (h + 1) * HEAD_DIM)
                o_ref[:, cols] = (acc_sc[:, cols] / l_sc[h]).astype(o_ref.dtype)
        else:
            acc_out[...] = acc_sc[...]
            stats_out[...] = jnp.zeros(stats_out.shape, jnp.float32)
            for h in range(heads):
                stats_out[:, h:h + 1] = m_sc[h][:, 0:1]
                stats_out[:, STATS_HALF + h:STATS_HALF + h + 1] = l_sc[h][:, 0:1]


def window_attention(query_normed, paired, ids, counts, state, last):
    rows, width = query_normed.shape
    local_tiles = rows // TILE_TOKENS
    heads = width // HEAD_DIM
    steps = WINDOW_SLOTS // SLOTS_PER_STEP
    first = state is None

    def window_spec(lead, sub):
        return pl.BlockSpec(
            (1, TILE_TOKENS, width),
            lambda t, j, ids, cnt: (lead, ids[t * WINDOW_SLOTS + j * SLOTS_PER_STEP + sub], 0),
        )

    row_spec = pl.BlockSpec((TILE_TOKENS, width), lambda t, j, ids, cnt: (t, 0))
    stats_spec = pl.BlockSpec((TILE_TOKENS, 2 * STATS_HALF), lambda t, j, ids, cnt: (t, 0))
    in_specs = [row_spec]
    in_specs += [window_spec(0, sub) for sub in range(SLOTS_PER_STEP)]
    in_specs += [window_spec(1, sub) for sub in range(SLOTS_PER_STEP)]
    operands = [ids, counts, query_normed] + [paired] * (2 * SLOTS_PER_STEP)
    if not first:
        in_specs += [row_spec, stats_spec]
        operands += list(state)
    if last:
        out_specs = pl.BlockSpec((TILE_TOKENS, width), lambda t, j, ids, cnt: (t, 0))
        out_shape = jax.ShapeDtypeStruct((rows, width), jnp.bfloat16)
    else:
        out_specs = [row_spec, stats_spec]
        out_shape = [
            jax.ShapeDtypeStruct((rows, width), jnp.float32),
            jax.ShapeDtypeStruct((rows, 2 * STATS_HALF), jnp.float32),
        ]
    grid_spec = pltpu.PrefetchScalarGridSpec(
        num_scalar_prefetch=2,
        grid=(local_tiles, steps),
        in_specs=in_specs,
        out_specs=out_specs,
        scratch_shapes=[
            pltpu.VMEM((heads, TILE_TOKENS, HEAD_DIM), jnp.float32),
            pltpu.VMEM((heads, TILE_TOKENS, HEAD_DIM), jnp.float32),
            pltpu.VMEM((TILE_TOKENS, width), jnp.float32),
        ],
    )
    return pl.pallas_call(
        functools.partial(attention_kernel, first=first, last=last),
        grid_spec=grid_spec,
        out_shape=out_shape,
        compiler_params=pltpu.CompilerParams(
            dimension_semantics=("arbitrary", "arbitrary")
        ),
    )(*operands)


def phase_windows(windows, local_tiles, phase, per_phase, tile_count):
    safe = jnp.clip(windows, 0, tile_count - 1)
    position = safe % local_tiles
    inside = (windows >= 0) & (position // per_phase == phase)
    block = (safe // local_tiles) * per_phase + position % per_phase
    order = jnp.argsort(jnp.logical_not(inside).astype(jnp.int32), axis=1, stable=True)
    ids = jnp.take_along_axis(block, order, axis=1)
    counts = jnp.sum(inside.astype(jnp.int32), axis=1)
    last = jnp.take_along_axis(ids, jnp.maximum(counts - 1, 0)[:, None], axis=1)
    slot = lax.broadcasted_iota(jnp.int32, ids.shape, 1)
    ids = jnp.where(slot < counts[:, None], ids, last)
    ids = jnp.clip(ids, 0, (tile_count // local_tiles) * per_phase - 1)
    return ids.reshape(-1).astype(jnp.int32), counts.astype(jnp.int32)


def on_device(query_states, key_states, value_states, query_gain, key_gain, windows, tok_count):
    rows = query_states.shape[0]
    local_tiles = rows // TILE_TOKENS
    tile_count = tok_count * local_tiles
    phases = 3 if local_tiles % 3 == 0 else 1
    per_phase = local_tiles // phases
    query_total, key_total = lax.psum((square_sums(query_states), square_sums(key_states)), "head")
    query_normed = normalize_rows(query_states, query_total, query_gain)
    sent_keys = normalize_rows(key_states, key_total, key_gain)
    state = None
    for phase in range(phases):
        part = slice(phase * per_phase * TILE_TOKENS, (phase + 1) * per_phase * TILE_TOKENS)
        paired = jnp.stack([sent_keys[part], value_states[part]])
        extended = lax.all_gather(paired, "tok", axis=1, tiled=True)
        ids, counts = phase_windows(windows, local_tiles, phase, per_phase, tile_count)
        state = window_attention(
            query_normed, extended, ids, counts, state, phase == phases - 1
        )
    return state


def solution(mesh):
    in_specs = (
        P("tok", "head"),
        P("tok", "head"),
        P("tok", "head"),
        P("head"),
        P("head"),
        P("tok", None),
    )
    out_specs = P("tok", "head")
    return jax.shard_map(
        functools.partial(on_device, tok_count=mesh.shape["tok"]),
        mesh=mesh,
        in_specs=in_specs,
        out_specs=out_specs,
        check_vma=False,
    )
```

```python
import functools
import math

import jax
import jax.numpy as jnp
from jax import lax
from jax.experimental import pallas as pl
from jax.experimental.pallas import tpu as pltpu
from jax.sharding import PartitionSpec as P

HEAD_DIM = 128
MODEL_DIM = 3072
TILE_TOKENS = 256
WINDOW_SLOTS = 27
SLOTS_PER_STEP = 1
STATS_HALF = 64


def square_sums(source):
    widened = source.astype(jnp.float32)
    return jnp.sum(widened * widened, axis=1)


def normalize_rows(source, totals, scale_gain):
    widened = source.astype(jnp.float32)
    return (widened * lax.rsqrt(totals[:, None] / MODEL_DIM + 1e-06) * scale_gain).astype(
        jnp.bfloat16
    )


def compact_windows(windows, tile_count):
    valid = windows >= 0
    order = jnp.argsort(jnp.logical_not(valid).astype(jnp.int32), axis=1, stable=True)
    ids = jnp.take_along_axis(windows, order, axis=1)
    counts = jnp.sum(valid.astype(jnp.int32), axis=1)
    last = jnp.take_along_axis(ids, jnp.maximum(counts - 1, 0)[:, None], axis=1)
    slot = lax.broadcasted_iota(jnp.int32, ids.shape, 1)
    ids = jnp.where(slot < counts[:, None], ids, last)
    ids = jnp.clip(ids, 0, tile_count - 1)
    return ids.reshape(-1).astype(jnp.int32), counts.astype(jnp.int32)


def attention_kernel(ids_ref, cnt_ref, q_ref, *refs, first, last):
    k_refs = refs[:SLOTS_PER_STEP]
    v_refs = refs[SLOTS_PER_STEP:2 * SLOTS_PER_STEP]
    rest = refs[2 * SLOTS_PER_STEP:]
    if not first:
        acc_in, stats_in = rest[:2]
        rest = rest[2:]
    if last:
        o_ref = rest[0]
        rest = rest[1:]
    else:
        acc_out, stats_out = rest[:2]
        rest = rest[2:]
    m_sc, l_sc, acc_sc = rest
    t = pl.program_id(0)
    j = pl.program_id(1)
    heads = q_ref.shape[1] // HEAD_DIM
    score_scale = 1.0 / math.sqrt(HEAD_DIM)

    @pl.when(j == 0)
    def _init():
        if first:
            m_sc[...] = jnp.full(m_sc.shape, -jnp.inf, jnp.float32)
            l_sc[...] = jnp.zeros(l_sc.shape, jnp.float32)
            acc_sc[...] = jnp.zeros(acc_sc.shape, jnp.float32)
        else:
            for h in range(heads):
                m_sc[h] = jnp.broadcast_to(stats_in[:, h:h + 1], m_sc.shape[1:])
                l_sc[h] = jnp.broadcast_to(
                    stats_in[:, STATS_HALF + h:STATS_HALF + h + 1], l_sc.shape[1:]
                )
            acc_sc[...] = acc_in[...]

    for sub in range(SLOTS_PER_STEP):
        k_ref = k_refs[sub]
        v_ref = v_refs[sub]

        @pl.when(j * SLOTS_PER_STEP + sub < cnt_ref[t])
        def _step():
            for h in range(heads):
                cols = slice(h * HEAD_DIM, (h + 1) * HEAD_DIM)
                q = q_ref[:, cols]
                k = k_ref[0, :, cols]
                v = v_ref[0, :, cols]
                scores = (
                    lax.dot_general(
                        q, k, (((1,), (1,)), ((), ())), preferred_element_type=jnp.float32
                    )
                    * score_scale
                )
                m_prev = m_sc[h]
                m_cur = jnp.max(scores, axis=1, keepdims=True)
                m_new = jnp.maximum(m_prev, m_cur)
                alpha = jnp.exp(m_prev - m_new)
                weights = jnp.exp(scores - m_new[:, :1])
                l_sc[h] = alpha * l_sc[h] + jnp.sum(weights, axis=1, keepdims=True)
                m_sc[h] = m_new
                mixed = jnp.dot(
                    weights.astype(jnp.bfloat16), v, preferred_element_type=jnp.float32
                )
                acc_sc[:, cols] = acc_sc[:, cols] * alpha + mixed

    @pl.when(j == pl.num_programs(1) - 1)
    def _finish():
        if last:
            for h in range(heads):
                cols = slice(h * HEAD_DIM, (h + 1) * HEAD_DIM)
                o_ref[:, cols] = (acc_sc[:, cols] / l_sc[h]).astype(o_ref.dtype)
        else:
            acc_out[...] = acc_sc[...]
            stats_out[...] = jnp.zeros(stats_out.shape, jnp.float32)
            for h in range(heads):
                stats_out[:, h:h + 1] = m_sc[h][:, 0:1]
                stats_out[:, STATS_HALF + h:STATS_HALF + h + 1] = l_sc[h][:, 0:1]


def window_attention(query_normed, paired, ids, counts, state, last):
    rows, width = query_normed.shape
    local_tiles = rows // TILE_TOKENS
    heads = width // HEAD_DIM
    steps = WINDOW_SLOTS // SLOTS_PER_STEP
    first = state is None

    def window_spec(lead, sub):
        return pl.BlockSpec(
            (1, TILE_TOKENS, width),
            lambda t, j, ids, cnt: (lead, ids[t * WINDOW_SLOTS + j * SLOTS_PER_STEP + sub], 0),
        )

    row_spec = pl.BlockSpec((TILE_TOKENS, width), lambda t, j, ids, cnt: (t, 0))
    stats_spec = pl.BlockSpec((TILE_TOKENS, 2 * STATS_HALF), lambda t, j, ids, cnt: (t, 0))
    in_specs = [row_spec]
    in_specs += [window_spec(0, sub) for sub in range(SLOTS_PER_STEP)]
    in_specs += [window_spec(1, sub) for sub in range(SLOTS_PER_STEP)]
    operands = [ids, counts, query_normed] + [paired] * (2 * SLOTS_PER_STEP)
    if not first:
        in_specs += [row_spec, stats_spec]
        operands += list(state)
    if last:
        out_specs = pl.BlockSpec((TILE_TOKENS, width), lambda t, j, ids, cnt: (t, 0))
        out_shape = jax.ShapeDtypeStruct((rows, width), jnp.bfloat16)
    else:
        out_specs = [row_spec, stats_spec]
        out_shape = [
            jax.ShapeDtypeStruct((rows, width), jnp.float32),
            jax.ShapeDtypeStruct((rows, 2 * STATS_HALF), jnp.float32),
        ]
    grid_spec = pltpu.PrefetchScalarGridSpec(
        num_scalar_prefetch=2,
        grid=(local_tiles, steps),
        in_specs=in_specs,
        out_specs=out_specs,
        scratch_shapes=[
            pltpu.VMEM((heads, TILE_TOKENS, HEAD_DIM), jnp.float32),
            pltpu.VMEM((heads, TILE_TOKENS, HEAD_DIM), jnp.float32),
            pltpu.VMEM((TILE_TOKENS, width), jnp.float32),
        ],
    )
    return pl.pallas_call(
        functools.partial(attention_kernel, first=first, last=last),
        grid_spec=grid_spec,
        out_shape=out_shape,
        compiler_params=pltpu.CompilerParams(
            dimension_semantics=("arbitrary", "arbitrary")
        ),
    )(*operands)


def phase_windows(windows, local_tiles, phase, per_phase, tile_count):
    safe = jnp.clip(windows, 0, tile_count - 1)
    position = safe % local_tiles
    inside = (windows >= 0) & (position // per_phase == phase)
    block = (safe // local_tiles) * per_phase + position % per_phase
    order = jnp.argsort(jnp.logical_not(inside).astype(jnp.int32), axis=1, stable=True)
    ids = jnp.take_along_axis(block, order, axis=1)
    counts = jnp.sum(inside.astype(jnp.int32), axis=1)
    last = jnp.take_along_axis(ids, jnp.maximum(counts - 1, 0)[:, None], axis=1)
    slot = lax.broadcasted_iota(jnp.int32, ids.shape, 1)
    ids = jnp.where(slot < counts[:, None], ids, last)
    ids = jnp.clip(ids, 0, (tile_count // local_tiles) * per_phase - 1)
    return ids.reshape(-1).astype(jnp.int32), counts.astype(jnp.int32)


def on_device(query_states, key_states, value_states, query_gain, key_gain, windows, tok_count):
    rows = query_states.shape[0]
    local_tiles = rows // TILE_TOKENS
    tile_count = tok_count * local_tiles
    phases = 3 if local_tiles % 3 == 0 else 1
    per_phase = local_tiles // phases
    query_total, key_total = lax.psum((square_sums(query_states), square_sums(key_states)), "head")
    query_normed = normalize_rows(query_states, query_total, query_gain)
    sent_keys = normalize_rows(key_states, key_total, key_gain)
    state = None
    for phase in range(phases):
        part = slice(phase * per_phase * TILE_TOKENS, (phase + 1) * per_phase * TILE_TOKENS)
        paired = jnp.stack([sent_keys[part], value_states[part]])
        extended = lax.all_gather(paired, "tok", axis=1, tiled=True)
        ids, counts = phase_windows(windows, local_tiles, phase, per_phase, tile_count)
        state = window_attention(
            query_normed, extended, ids, counts, state, phase == phases - 1
        )
    return state


def solution(mesh):
    in_specs = (
        P("tok", "head"),
        P("tok", "head"),
        P("tok", "head"),
        P("head"),
        P("head"),
        P("tok", None),
    )
    out_specs = P("tok", "head")
    return jax.shard_map(
        functools.partial(on_device, tok_count=mesh.shape["tok"]),
        mesh=mesh,
        in_specs=in_specs,
        out_specs=out_specs,
        check_vma=False,
    )
```

```python
import functools
import math

import jax
import jax.numpy as jnp
from jax import lax
from jax.experimental import pallas as pl
from jax.experimental.pallas import tpu as pltpu
from jax.sharding import PartitionSpec as P

HEAD_DIM = 128
MODEL_DIM = 3072
TILE_TOKENS = 256
WINDOW_SLOTS = 27
SLOTS_PER_STEP = 1
STATS_HALF = 64


def square_sums(source):
    widened = source.astype(jnp.float32)
    return jnp.sum(widened * widened, axis=1)


def normalize_rows(source, totals, scale_gain):
    widened = source.astype(jnp.float32)
    return (widened * lax.rsqrt(totals[:, None] / MODEL_DIM + 1e-06) * scale_gain).astype(
        jnp.bfloat16
    )


def compact_windows(windows, tile_count):
    valid = windows >= 0
    order = jnp.argsort(jnp.logical_not(valid).astype(jnp.int32), axis=1, stable=True)
    ids = jnp.take_along_axis(windows, order, axis=1)
    counts = jnp.sum(valid.astype(jnp.int32), axis=1)
    last = jnp.take_along_axis(ids, jnp.maximum(counts - 1, 0)[:, None], axis=1)
    slot = lax.broadcasted_iota(jnp.int32, ids.shape, 1)
    ids = jnp.where(slot < counts[:, None], ids, last)
    ids = jnp.clip(ids, 0, tile_count - 1)
    return ids.reshape(-1).astype(jnp.int32), counts.astype(jnp.int32)


def attention_kernel(ids_ref, cnt_ref, q_ref, *refs, first, last):
    k_refs = refs[:SLOTS_PER_STEP]
    v_refs = refs[SLOTS_PER_STEP:2 * SLOTS_PER_STEP]
    rest = refs[2 * SLOTS_PER_STEP:]
    if not first:
        acc_in, stats_in = rest[:2]
        rest = rest[2:]
    if last:
        o_ref = rest[0]
        rest = rest[1:]
    else:
        acc_out, stats_out = rest[:2]
        rest = rest[2:]
    m_sc, l_sc, acc_sc = rest
    t = pl.program_id(0)
    j = pl.program_id(1)
    heads = q_ref.shape[0] // HEAD_DIM
    score_scale = 1.0 / math.sqrt(HEAD_DIM)

    @pl.when(j == 0)
    def _init():
        if first:
            m_sc[...] = jnp.full(m_sc.shape, -jnp.inf, jnp.float32)
            l_sc[...] = jnp.zeros(l_sc.shape, jnp.float32)
            acc_sc[...] = jnp.zeros(acc_sc.shape, jnp.float32)
        else:
            m_sc[...] = stats_in[0, 0]
            l_sc[...] = stats_in[0, 1]
            acc_sc[...] = acc_in[0]

    for sub in range(SLOTS_PER_STEP):
        k_ref = k_refs[sub]
        v_ref = v_refs[sub]

        @pl.when(j * SLOTS_PER_STEP + sub < cnt_ref[t])
        def _step():
            for h in range(heads):
                cols = slice(h * HEAD_DIM, (h + 1) * HEAD_DIM)
                q_t = q_ref[cols, :]
                k = k_ref[0, :, cols]
                v = v_ref[0, :, cols]
                scores = (
                    lax.dot_general(
                        k, q_t, (((1,), (0,)), ((), ())), preferred_element_type=jnp.float32
                    )
                    * score_scale
                )
                m_prev = m_sc[h]
                m_cur = jnp.max(scores, axis=0, keepdims=True)
                m_new = jnp.maximum(m_prev, m_cur)
                alpha = jnp.exp(m_prev - m_new)
                weights = jnp.exp(scores - m_new)
                l_sc[h] = alpha * l_sc[h] + jnp.sum(weights, axis=0, keepdims=True)
                m_sc[h] = m_new
                mixed = lax.dot_general(
                    v, weights.astype(jnp.bfloat16), (((0,), (0,)), ((), ())),
                    preferred_element_type=jnp.float32,
                )
                acc_sc[cols, :] = acc_sc[cols, :] * alpha + mixed

    @pl.when(j == pl.num_programs(1) - 1)
    def _finish():
        if last:
            for h in range(heads):
                cols = slice(h * HEAD_DIM, (h + 1) * HEAD_DIM)
                o_ref[:, cols] = (acc_sc[cols, :] / l_sc[h]).T.astype(o_ref.dtype)
        else:
            acc_out[0] = acc_sc[...]
            stats_out[0, 0] = m_sc[...]
            stats_out[0, 1] = l_sc[...]


def window_attention(query_t, paired, ids, counts, state, last):
    width, rows = query_t.shape
    local_tiles = rows // TILE_TOKENS
    heads = width // HEAD_DIM
    steps = WINDOW_SLOTS // SLOTS_PER_STEP
    first = state is None

    def window_spec(lead, sub):
        return pl.BlockSpec(
            (1, TILE_TOKENS, width),
            lambda t, j, ids, cnt: (lead, ids[t * WINDOW_SLOTS + j * SLOTS_PER_STEP + sub], 0),
        )

    acc_spec = pl.BlockSpec((1, width, TILE_TOKENS), lambda t, j, ids, cnt: (t, 0, 0))
    stats_spec = pl.BlockSpec(
        (1, 2, heads, 1, TILE_TOKENS), lambda t, j, ids, cnt: (t, 0, 0, 0, 0)
    )
    in_specs = [pl.BlockSpec((width, TILE_TOKENS), lambda t, j, ids, cnt: (0, t))]
    in_specs += [window_spec(0, sub) for sub in range(SLOTS_PER_STEP)]
    in_specs += [window_spec(1, sub) for sub in range(SLOTS_PER_STEP)]
    operands = [ids, counts, query_t] + [paired] * (2 * SLOTS_PER_STEP)
    if not first:
        in_specs += [acc_spec, stats_spec]
        operands += list(state)
    if last:
        out_specs = pl.BlockSpec((TILE_TOKENS, width), lambda t, j, ids, cnt: (t, 0))
        out_shape = jax.ShapeDtypeStruct((rows, width), jnp.bfloat16)
    else:
        out_specs = [acc_spec, stats_spec]
        out_shape = [
            jax.ShapeDtypeStruct((local_tiles, width, TILE_TOKENS), jnp.float32),
            jax.ShapeDtypeStruct((local_tiles, 2, heads, 1, TILE_TOKENS), jnp.float32),
        ]
    grid_spec = pltpu.PrefetchScalarGridSpec(
        num_scalar_prefetch=2,
        grid=(local_tiles, steps),
        in_specs=in_specs,
        out_specs=out_specs,
        scratch_shapes=[
            pltpu.VMEM((heads, 1, TILE_TOKENS), jnp.float32),
            pltpu.VMEM((heads, 1, TILE_TOKENS), jnp.float32),
            pltpu.VMEM((width, TILE_TOKENS), jnp.float32),
        ],
    )
    return pl.pallas_call(
        functools.partial(attention_kernel, first=first, last=last),
        grid_spec=grid_spec,
        out_shape=out_shape,
        compiler_params=pltpu.CompilerParams(
            dimension_semantics=("arbitrary", "arbitrary")
        ),
    )(*operands)


def phase_windows(windows, local_tiles, phase, per_phase, tile_count):
    safe = jnp.clip(windows, 0, tile_count - 1)
    position = safe % local_tiles
    inside = (windows >= 0) & (position // per_phase == phase)
    block = (safe // local_tiles) * per_phase + position % per_phase
    order = jnp.argsort(jnp.logical_not(inside).astype(jnp.int32), axis=1, stable=True)
    ids = jnp.take_along_axis(block, order, axis=1)
    counts = jnp.sum(inside.astype(jnp.int32), axis=1)
    last = jnp.take_along_axis(ids, jnp.maximum(counts - 1, 0)[:, None], axis=1)
    slot = lax.broadcasted_iota(jnp.int32, ids.shape, 1)
    ids = jnp.where(slot < counts[:, None], ids, last)
    ids = jnp.clip(ids, 0, (tile_count // local_tiles) * per_phase - 1)
    return ids.reshape(-1).astype(jnp.int32), counts.astype(jnp.int32)


def on_device(query_states, key_states, value_states, query_gain, key_gain, windows, tok_count):
    rows = query_states.shape[0]
    local_tiles = rows // TILE_TOKENS
    tile_count = tok_count * local_tiles
    phases = 3 if local_tiles % 3 == 0 else 1
    per_phase = local_tiles // phases
    query_total, key_total = lax.psum((square_sums(query_states), square_sums(key_states)), "head")
    query_normed = normalize_rows(query_states, query_total, query_gain)
    sent_keys = normalize_rows(key_states, key_total, key_gain)
    query_t = query_normed.T
    state = None
    for phase in range(phases):
        part = slice(phase * per_phase * TILE_TOKENS, (phase + 1) * per_phase * TILE_TOKENS)
        paired = jnp.stack([sent_keys[part], value_states[part]])
        extended = lax.all_gather(paired, "tok", axis=1, tiled=True)
        ids, counts = phase_windows(windows, local_tiles, phase, per_phase, tile_count)
        state = window_attention(
            query_t, extended, ids, counts, state, phase == phases - 1
        )
    return state


def solution(mesh):
    in_specs = (
        P("tok", "head"),
        P("tok", "head"),
        P("tok", "head"),
        P("head"),
        P("head"),
        P("tok", None),
    )
    out_specs = P("tok", "head")
    return jax.shard_map(
        functools.partial(on_device, tok_count=mesh.shape["tok"]),
        mesh=mesh,
        in_specs=in_specs,
        out_specs=out_specs,
        check_vma=False,
    )
```

```python
import functools
import math

import jax
import jax.numpy as jnp
from jax import lax
from jax.experimental import pallas as pl
from jax.experimental.pallas import tpu as pltpu
from jax.sharding import PartitionSpec as P

HEAD_DIM = 128
MODEL_DIM = 3072
TILE_TOKENS = 256
WINDOW_SLOTS = 27
SLOTS_PER_STEP = 1
STATS_HALF = 64


def square_sums(source):
    widened = source.astype(jnp.float32)
    return jnp.sum(widened * widened, axis=1)


def normalize_rows(source, totals, scale_gain):
    widened = source.astype(jnp.float32)
    return (widened * lax.rsqrt(totals[:, None] / MODEL_DIM + 1e-06) * scale_gain).astype(
        jnp.bfloat16
    )


def compact_windows(windows, tile_count):
    valid = windows >= 0
    order = jnp.argsort(jnp.logical_not(valid).astype(jnp.int32), axis=1, stable=True)
    ids = jnp.take_along_axis(windows, order, axis=1)
    counts = jnp.sum(valid.astype(jnp.int32), axis=1)
    last = jnp.take_along_axis(ids, jnp.maximum(counts - 1, 0)[:, None], axis=1)
    slot = lax.broadcasted_iota(jnp.int32, ids.shape, 1)
    ids = jnp.where(slot < counts[:, None], ids, last)
    ids = jnp.clip(ids, 0, tile_count - 1)
    return ids.reshape(-1).astype(jnp.int32), counts.astype(jnp.int32)


def attention_kernel(ids_ref, cnt_ref, q_ref, *refs, first, last):
    k_refs = refs[:SLOTS_PER_STEP]
    v_refs = refs[SLOTS_PER_STEP:2 * SLOTS_PER_STEP]
    rest = refs[2 * SLOTS_PER_STEP:]
    if not first:
        acc_in, stats_in = rest[:2]
        rest = rest[2:]
    if last:
        o_ref = rest[0]
        rest = rest[1:]
    else:
        acc_out, stats_out = rest[:2]
        rest = rest[2:]
    m_sc, l_sc, acc_sc = rest
    t = pl.program_id(0)
    j = pl.program_id(1)
    heads = q_ref.shape[0] // HEAD_DIM
    score_scale = 1.0 / math.sqrt(HEAD_DIM)

    @pl.when(j == 0)
    def _init():
        if first:
            m_sc[...] = jnp.full(m_sc.shape, -jnp.inf, jnp.float32)
            l_sc[...] = jnp.zeros(l_sc.shape, jnp.float32)
            acc_sc[...] = jnp.zeros(acc_sc.shape, jnp.float32)
        else:
            m_sc[...] = stats_in[0, 0]
            l_sc[...] = stats_in[0, 1]
            acc_sc[...] = acc_in[0]

    for sub in range(SLOTS_PER_STEP):
        k_ref = k_refs[sub]
        v_ref = v_refs[sub]

        @pl.when(j * SLOTS_PER_STEP + sub < cnt_ref[t])
        def _step():
            for h in range(heads):
                cols = slice(h * HEAD_DIM, (h + 1) * HEAD_DIM)
                q_t = q_ref[cols, :]
                k = k_ref[0, :, cols]
                v = v_ref[0, :, cols]
                scores = (
                    lax.dot_general(
                        k, q_t, (((1,), (0,)), ((), ())), preferred_element_type=jnp.float32
                    )
                    * score_scale
                )
                m_prev = m_sc[h]
                m_cur = jnp.max(scores, axis=0, keepdims=True)
                m_new = jnp.maximum(m_prev, m_cur)
                alpha = jnp.exp(m_prev - m_new)
                weights = jnp.exp(scores - m_new)
                l_sc[h] = alpha * l_sc[h] + jnp.sum(weights, axis=0, keepdims=True)
                m_sc[h] = m_new
                mixed = lax.dot_general(
                    v, weights.astype(jnp.bfloat16), (((0,), (0,)), ((), ())),
                    preferred_element_type=jnp.float32,
                )
                acc_sc[cols, :] = acc_sc[cols, :] * alpha + mixed

    @pl.when(j == pl.num_programs(1) - 1)
    def _finish():
        if last:
            for h in range(heads):
                cols = slice(h * HEAD_DIM, (h + 1) * HEAD_DIM)
                o_ref[:, cols] = (acc_sc[cols, :] / l_sc[h]).T.astype(o_ref.dtype)
        else:
            acc_out[0] = acc_sc[...]
            stats_out[0, 0] = m_sc[...]
            stats_out[0, 1] = l_sc[...]


def window_attention(query_t, paired, ids, counts, state, last):
    width, rows = query_t.shape
    local_tiles = rows // TILE_TOKENS
    heads = width // HEAD_DIM
    steps = WINDOW_SLOTS // SLOTS_PER_STEP
    first = state is None

    def window_spec(lead, sub):
        return pl.BlockSpec(
            (1, TILE_TOKENS, width),
            lambda t, j, ids, cnt: (lead, ids[t * WINDOW_SLOTS + j * SLOTS_PER_STEP + sub], 0),
        )

    acc_spec = pl.BlockSpec((1, width, TILE_TOKENS), lambda t, j, ids, cnt: (t, 0, 0))
    stats_spec = pl.BlockSpec(
        (1, 2, heads, 1, TILE_TOKENS), lambda t, j, ids, cnt: (t, 0, 0, 0, 0)
    )
    in_specs = [pl.BlockSpec((width, TILE_TOKENS), lambda t, j, ids, cnt: (0, t))]
    in_specs += [window_spec(0, sub) for sub in range(SLOTS_PER_STEP)]
    in_specs += [window_spec(1, sub) for sub in range(SLOTS_PER_STEP)]
    operands = [ids, counts, query_t] + [paired] * (2 * SLOTS_PER_STEP)
    if not first:
        in_specs += [acc_spec, stats_spec]
        operands += list(state)
    if last:
        out_specs = pl.BlockSpec((TILE_TOKENS, width), lambda t, j, ids, cnt: (t, 0))
        out_shape = jax.ShapeDtypeStruct((rows, width), jnp.bfloat16)
    else:
        out_specs = [acc_spec, stats_spec]
        out_shape = [
            jax.ShapeDtypeStruct((local_tiles, width, TILE_TOKENS), jnp.float32),
            jax.ShapeDtypeStruct((local_tiles, 2, heads, 1, TILE_TOKENS), jnp.float32),
        ]
    grid_spec = pltpu.PrefetchScalarGridSpec(
        num_scalar_prefetch=2,
        grid=(local_tiles, steps),
        in_specs=in_specs,
        out_specs=out_specs,
        scratch_shapes=[
            pltpu.VMEM((heads, 1, TILE_TOKENS), jnp.float32),
            pltpu.VMEM((heads, 1, TILE_TOKENS), jnp.float32),
            pltpu.VMEM((width, TILE_TOKENS), jnp.float32),
        ],
    )
    return pl.pallas_call(
        functools.partial(attention_kernel, first=first, last=last),
        grid_spec=grid_spec,
        out_shape=out_shape,
        compiler_params=pltpu.CompilerParams(
            dimension_semantics=("arbitrary", "arbitrary")
        ),
    )(*operands)


def phase_windows(windows, local_tiles, start, size, tile_count):
    safe = jnp.clip(windows, 0, tile_count - 1)
    position = safe % local_tiles
    inside = (windows >= 0) & (position >= start) & (position < start + size)
    block = (safe // local_tiles) * size + jnp.clip(position - start, 0, size - 1)
    order = jnp.argsort(jnp.logical_not(inside).astype(jnp.int32), axis=1, stable=True)
    ids = jnp.take_along_axis(block, order, axis=1)
    counts = jnp.sum(inside.astype(jnp.int32), axis=1)
    last = jnp.take_along_axis(ids, jnp.maximum(counts - 1, 0)[:, None], axis=1)
    slot = lax.broadcasted_iota(jnp.int32, ids.shape, 1)
    ids = jnp.where(slot < counts[:, None], ids, last)
    ids = jnp.clip(ids, 0, (tile_count // local_tiles) * size - 1)
    return ids.reshape(-1).astype(jnp.int32), counts.astype(jnp.int32)


def phase_sizes(local_tiles):
    if local_tiles % 2 == 0 and local_tiles >= 4:
        return [2] * (local_tiles // 2 - 1) + [1, 1]
    return [local_tiles]


def on_device(query_states, key_states, value_states, query_gain, key_gain, windows, tok_count):
    rows = query_states.shape[0]
    local_tiles = rows // TILE_TOKENS
    tile_count = tok_count * local_tiles
    sizes = phase_sizes(local_tiles)
    query_total, key_total = lax.psum((square_sums(query_states), square_sums(key_states)), "head")
    query_normed = normalize_rows(query_states, query_total, query_gain)
    sent_keys = normalize_rows(key_states, key_total, key_gain)
    query_t = query_normed.T
    state = None
    start = 0
    for number, size in enumerate(sizes):
        part = slice(start * TILE_TOKENS, (start + size) * TILE_TOKENS)
        paired = jnp.stack([sent_keys[part], value_states[part]])
        extended = lax.all_gather(paired, "tok", axis=1, tiled=True)
        ids, counts = phase_windows(windows, local_tiles, start, size, tile_count)
        state = window_attention(
            query_t, extended, ids, counts, state, number == len(sizes) - 1
        )
        start += size
    return state


def solution(mesh):
    in_specs = (
        P("tok", "head"),
        P("tok", "head"),
        P("tok", "head"),
        P("head"),
        P("head"),
        P("tok", None),
    )
    out_specs = P("tok", "head")
    return jax.shard_map(
        functools.partial(on_device, tok_count=mesh.shape["tok"]),
        mesh=mesh,
        in_specs=in_specs,
        out_specs=out_specs,
        check_vma=False,
    )
```

```python
import functools
import math

import jax
import jax.numpy as jnp
from jax import lax
from jax.experimental import pallas as pl
from jax.experimental.pallas import tpu as pltpu
from jax.sharding import PartitionSpec as P

HEAD_DIM = 128
MODEL_DIM = 3072
TILE_TOKENS = 256
WINDOW_SLOTS = 27
SLOTS_PER_STEP = 1
STATS_HALF = 64


def square_sums(source):
    widened = source.astype(jnp.float32)
    return jnp.sum(widened * widened, axis=1)


def normalize_rows(source, totals, scale_gain):
    widened = source.astype(jnp.float32)
    return (widened * lax.rsqrt(totals[:, None] / MODEL_DIM + 1e-06) * scale_gain).astype(
        jnp.bfloat16
    )


def compact_windows(windows, tile_count):
    valid = windows >= 0
    order = jnp.argsort(jnp.logical_not(valid).astype(jnp.int32), axis=1, stable=True)
    ids = jnp.take_along_axis(windows, order, axis=1)
    counts = jnp.sum(valid.astype(jnp.int32), axis=1)
    last = jnp.take_along_axis(ids, jnp.maximum(counts - 1, 0)[:, None], axis=1)
    slot = lax.broadcasted_iota(jnp.int32, ids.shape, 1)
    ids = jnp.where(slot < counts[:, None], ids, last)
    ids = jnp.clip(ids, 0, tile_count - 1)
    return ids.reshape(-1).astype(jnp.int32), counts.astype(jnp.int32)


def attention_kernel(ids_ref, cnt_ref, q_ref, *refs, first, last):
    k_refs = refs[:SLOTS_PER_STEP]
    v_refs = refs[SLOTS_PER_STEP:2 * SLOTS_PER_STEP]
    rest = refs[2 * SLOTS_PER_STEP:]
    if not first:
        acc_in, stats_in = rest[:2]
        rest = rest[2:]
    if last:
        o_ref = rest[0]
        rest = rest[1:]
    else:
        acc_out, stats_out = rest[:2]
        rest = rest[2:]
    m_sc, l_sc, acc_sc = rest
    t = pl.program_id(0)
    j = pl.program_id(1)
    heads = q_ref.shape[0] // HEAD_DIM
    score_scale = 1.0 / math.sqrt(HEAD_DIM)

    @pl.when(j == 0)
    def _init():
        if first:
            m_sc[...] = jnp.full(m_sc.shape, -jnp.inf, jnp.float32)
            l_sc[...] = jnp.zeros(l_sc.shape, jnp.float32)
            acc_sc[...] = jnp.zeros(acc_sc.shape, jnp.float32)
        else:
            m_sc[...] = stats_in[0, 0]
            l_sc[...] = stats_in[0, 1]
            acc_sc[...] = acc_in[0]

    for sub in range(SLOTS_PER_STEP):
        k_ref = k_refs[sub]
        v_ref = v_refs[sub]

        @pl.when(j * SLOTS_PER_STEP + sub < cnt_ref[t])
        def _step():
            for h in range(heads):
                cols = slice(h * HEAD_DIM, (h + 1) * HEAD_DIM)
                q_t = q_ref[cols, :]
                k = k_ref[0, :, cols]
                v = v_ref[0, :, cols]
                scores = (
                    lax.dot_general(
                        k, q_t, (((1,), (0,)), ((), ())), preferred_element_type=jnp.float32
                    )
                    * score_scale
                )
                m_prev = m_sc[h]
                m_cur = jnp.max(scores, axis=0, keepdims=True)
                m_new = jnp.maximum(m_prev, m_cur)
                alpha = jnp.exp(m_prev - m_new)
                weights = jnp.exp(scores - m_new)
                l_sc[h] = alpha * l_sc[h] + jnp.sum(weights, axis=0, keepdims=True)
                m_sc[h] = m_new
                mixed = lax.dot_general(
                    v, weights.astype(jnp.bfloat16), (((0,), (0,)), ((), ())),
                    preferred_element_type=jnp.float32,
                )
                acc_sc[cols, :] = acc_sc[cols, :] * alpha + mixed

    @pl.when(j == pl.num_programs(1) - 1)
    def _finish():
        if last:
            for h in range(heads):
                cols = slice(h * HEAD_DIM, (h + 1) * HEAD_DIM)
                o_ref[:, cols] = (acc_sc[cols, :] / l_sc[h]).T.astype(o_ref.dtype)
        else:
            acc_out[0] = acc_sc[...]
            stats_out[0, 0] = m_sc[...]
            stats_out[0, 1] = l_sc[...]


def window_attention(query_t, paired, ids, counts, state, last):
    width, rows = query_t.shape
    local_tiles = rows // TILE_TOKENS
    heads = width // HEAD_DIM
    steps = WINDOW_SLOTS // SLOTS_PER_STEP
    first = state is None

    def window_spec(lead, sub):
        return pl.BlockSpec(
            (1, TILE_TOKENS, width),
            lambda t, j, ids, cnt: (lead, ids[t * WINDOW_SLOTS + j * SLOTS_PER_STEP + sub], 0),
        )

    acc_spec = pl.BlockSpec((1, width, TILE_TOKENS), lambda t, j, ids, cnt: (t, 0, 0))
    stats_spec = pl.BlockSpec(
        (1, 2, heads, 1, TILE_TOKENS), lambda t, j, ids, cnt: (t, 0, 0, 0, 0)
    )
    in_specs = [pl.BlockSpec((width, TILE_TOKENS), lambda t, j, ids, cnt: (0, t))]
    in_specs += [window_spec(0, sub) for sub in range(SLOTS_PER_STEP)]
    in_specs += [window_spec(1, sub) for sub in range(SLOTS_PER_STEP)]
    operands = [ids, counts, query_t] + [paired] * (2 * SLOTS_PER_STEP)
    if not first:
        in_specs += [acc_spec, stats_spec]
        operands += list(state)
    if last:
        out_specs = pl.BlockSpec((TILE_TOKENS, width), lambda t, j, ids, cnt: (t, 0))
        out_shape = jax.ShapeDtypeStruct((rows, width), jnp.bfloat16)
    else:
        out_specs = [acc_spec, stats_spec]
        out_shape = [
            jax.ShapeDtypeStruct((local_tiles, width, TILE_TOKENS), jnp.float32),
            jax.ShapeDtypeStruct((local_tiles, 2, heads, 1, TILE_TOKENS), jnp.float32),
        ]
    grid_spec = pltpu.PrefetchScalarGridSpec(
        num_scalar_prefetch=2,
        grid=(local_tiles, steps),
        in_specs=in_specs,
        out_specs=out_specs,
        scratch_shapes=[
            pltpu.VMEM((heads, 1, TILE_TOKENS), jnp.float32),
            pltpu.VMEM((heads, 1, TILE_TOKENS), jnp.float32),
            pltpu.VMEM((width, TILE_TOKENS), jnp.float32),
        ],
    )
    return pl.pallas_call(
        functools.partial(attention_kernel, first=first, last=last),
        grid_spec=grid_spec,
        out_shape=out_shape,
        compiler_params=pltpu.CompilerParams(
            dimension_semantics=("arbitrary", "arbitrary")
        ),
    )(*operands)


def phase_windows(windows, local_tiles, start, size, tile_count):
    safe = jnp.clip(windows, 0, tile_count - 1)
    position = safe % local_tiles
    inside = (windows >= 0) & (position >= start) & (position < start + size)
    block = (safe // local_tiles) * size + jnp.clip(position - start, 0, size - 1)
    order = jnp.argsort(jnp.logical_not(inside).astype(jnp.int32), axis=1, stable=True)
    ids = jnp.take_along_axis(block, order, axis=1)
    counts = jnp.sum(inside.astype(jnp.int32), axis=1)
    last = jnp.take_along_axis(ids, jnp.maximum(counts - 1, 0)[:, None], axis=1)
    slot = lax.broadcasted_iota(jnp.int32, ids.shape, 1)
    ids = jnp.where(slot < counts[:, None], ids, last)
    ids = jnp.clip(ids, 0, (tile_count // local_tiles) * size - 1)
    return ids.reshape(-1).astype(jnp.int32), counts.astype(jnp.int32)


def phase_sizes(local_tiles):
    if local_tiles >= 3:
        return [1, 2] + [1] * (local_tiles - 3)
    return [local_tiles]


def on_device(query_states, key_states, value_states, query_gain, key_gain, windows, tok_count):
    rows = query_states.shape[0]
    local_tiles = rows // TILE_TOKENS
    tile_count = tok_count * local_tiles
    sizes = phase_sizes(local_tiles)
    query_total, key_total = lax.psum((square_sums(query_states), square_sums(key_states)), "head")
    query_normed = normalize_rows(query_states, query_total, query_gain)
    sent_keys = normalize_rows(key_states, key_total, key_gain)
    query_t = query_normed.T
    state = None
    start = 0
    for number, size in enumerate(sizes):
        part = slice(start * TILE_TOKENS, (start + size) * TILE_TOKENS)
        paired = jnp.stack([sent_keys[part], value_states[part]])
        extended = lax.all_gather(paired, "tok", axis=1, tiled=True)
        ids, counts = phase_windows(windows, local_tiles, start, size, tile_count)
        state = window_attention(
            query_t, extended, ids, counts, state, number == len(sizes) - 1
        )
        start += size
    return state


def solution(mesh):
    in_specs = (
        P("tok", "head"),
        P("tok", "head"),
        P("tok", "head"),
        P("head"),
        P("head"),
        P("tok", None),
    )
    out_specs = P("tok", "head")
    return jax.shard_map(
        functools.partial(on_device, tok_count=mesh.shape["tok"]),
        mesh=mesh,
        in_specs=in_specs,
        out_specs=out_specs,
        check_vma=False,
    )
```

```python
import functools
import math

import jax
import jax.numpy as jnp
from jax import lax
from jax.experimental import pallas as pl
from jax.experimental.pallas import tpu as pltpu
from jax.sharding import PartitionSpec as P

HEAD_DIM = 128
MODEL_DIM = 3072
TILE_TOKENS = 256
WINDOW_SLOTS = 27
FRAME_SLOTS = 9
FRAME_ROWS = 4
FRAME_COLS = 4
SLOTS_PER_STEP = 1
STATS_HALF = 64


def square_sums(source):
    widened = source.astype(jnp.float32)
    return jnp.sum(widened * widened, axis=1)


def normalize_rows(source, totals, scale_gain):
    widened = source.astype(jnp.float32)
    return (widened * lax.rsqrt(totals[:, None] / MODEL_DIM + 1e-06) * scale_gain).astype(
        jnp.bfloat16
    )


def compact_windows(windows, tile_count):
    valid = windows >= 0
    order = jnp.argsort(jnp.logical_not(valid).astype(jnp.int32), axis=1, stable=True)
    ids = jnp.take_along_axis(windows, order, axis=1)
    counts = jnp.sum(valid.astype(jnp.int32), axis=1)
    last = jnp.take_along_axis(ids, jnp.maximum(counts - 1, 0)[:, None], axis=1)
    slot = lax.broadcasted_iota(jnp.int32, ids.shape, 1)
    ids = jnp.where(slot < counts[:, None], ids, last)
    ids = jnp.clip(ids, 0, tile_count - 1)
    return ids.reshape(-1).astype(jnp.int32), counts.astype(jnp.int32)


def attention_kernel(ids_ref, cnt_ref, q_ref, *refs, first, last):
    k_refs = refs[:SLOTS_PER_STEP]
    v_refs = refs[SLOTS_PER_STEP:2 * SLOTS_PER_STEP]
    rest = refs[2 * SLOTS_PER_STEP:]
    if not first:
        acc_in, stats_in = rest[:2]
        rest = rest[2:]
    if last:
        o_ref = rest[0]
        rest = rest[1:]
    else:
        acc_out, stats_out = rest[:2]
        rest = rest[2:]
    m_sc, l_sc, acc_sc = rest
    t = pl.program_id(0)
    j = pl.program_id(1)
    heads = q_ref.shape[0] // HEAD_DIM
    score_scale = 1.0 / math.sqrt(HEAD_DIM)

    @pl.when(j == 0)
    def _init():
        if first:
            m_sc[...] = jnp.full(m_sc.shape, -jnp.inf, jnp.float32)
            l_sc[...] = jnp.zeros(l_sc.shape, jnp.float32)
            acc_sc[...] = jnp.zeros(acc_sc.shape, jnp.float32)
        else:
            m_sc[...] = stats_in[0, 0]
            l_sc[...] = stats_in[0, 1]
            acc_sc[...] = acc_in[0]

    for sub in range(SLOTS_PER_STEP):
        k_ref = k_refs[sub]
        v_ref = v_refs[sub]

        @pl.when(j * SLOTS_PER_STEP + sub < cnt_ref[t])
        def _step():
            for h in range(heads):
                cols = slice(h * HEAD_DIM, (h + 1) * HEAD_DIM)
                q_t = q_ref[cols, :]
                k = k_ref[0, :, cols]
                v = v_ref[0, :, cols]
                scores = (
                    lax.dot_general(
                        k, q_t, (((1,), (0,)), ((), ())), preferred_element_type=jnp.float32
                    )
                    * score_scale
                )
                m_prev = m_sc[h]
                m_cur = jnp.max(scores, axis=0, keepdims=True)
                m_new = jnp.maximum(m_prev, m_cur)
                alpha = jnp.exp(m_prev - m_new)
                weights = jnp.exp(scores - m_new)
                l_sc[h] = alpha * l_sc[h] + jnp.sum(weights, axis=0, keepdims=True)
                m_sc[h] = m_new
                mixed = lax.dot_general(
                    v, weights.astype(jnp.bfloat16), (((0,), (0,)), ((), ())),
                    preferred_element_type=jnp.float32,
                )
                acc_sc[cols, :] = acc_sc[cols, :] * alpha + mixed

    @pl.when(j == pl.num_programs(1) - 1)
    def _finish():
        if last:
            for h in range(heads):
                cols = slice(h * HEAD_DIM, (h + 1) * HEAD_DIM)
                o_ref[:, cols] = (acc_sc[cols, :] / l_sc[h]).T.astype(o_ref.dtype)
        else:
            acc_out[0] = acc_sc[...]
            stats_out[0, 0] = m_sc[...]
            stats_out[0, 1] = l_sc[...]


def window_attention(query_t, paired, ids, counts, state, last, bound):
    width, rows = query_t.shape
    local_tiles = rows // TILE_TOKENS
    heads = width // HEAD_DIM
    steps = bound // SLOTS_PER_STEP
    first = state is None

    def window_spec(lead, sub):
        return pl.BlockSpec(
            (1, TILE_TOKENS, width),
            lambda t, j, ids, cnt: (lead, ids[t * WINDOW_SLOTS + j * SLOTS_PER_STEP + sub], 0),
        )

    acc_spec = pl.BlockSpec((1, width, TILE_TOKENS), lambda t, j, ids, cnt: (t, 0, 0))
    stats_spec = pl.BlockSpec(
        (1, 2, heads, 1, TILE_TOKENS), lambda t, j, ids, cnt: (t, 0, 0, 0, 0)
    )
    in_specs = [pl.BlockSpec((width, TILE_TOKENS), lambda t, j, ids, cnt: (0, t))]
    in_specs += [window_spec(0, sub) for sub in range(SLOTS_PER_STEP)]
    in_specs += [window_spec(1, sub) for sub in range(SLOTS_PER_STEP)]
    operands = [ids, counts, query_t] + [paired] * (2 * SLOTS_PER_STEP)
    if not first:
        in_specs += [acc_spec, stats_spec]
        operands += list(state)
    if last:
        out_specs = pl.BlockSpec((TILE_TOKENS, width), lambda t, j, ids, cnt: (t, 0))
        out_shape = jax.ShapeDtypeStruct((rows, width), jnp.bfloat16)
    else:
        out_specs = [acc_spec, stats_spec]
        out_shape = [
            jax.ShapeDtypeStruct((local_tiles, width, TILE_TOKENS), jnp.float32),
            jax.ShapeDtypeStruct((local_tiles, 2, heads, 1, TILE_TOKENS), jnp.float32),
        ]
    grid_spec = pltpu.PrefetchScalarGridSpec(
        num_scalar_prefetch=2,
        grid=(local_tiles, steps),
        in_specs=in_specs,
        out_specs=out_specs,
        scratch_shapes=[
            pltpu.VMEM((heads, 1, TILE_TOKENS), jnp.float32),
            pltpu.VMEM((heads, 1, TILE_TOKENS), jnp.float32),
            pltpu.VMEM((width, TILE_TOKENS), jnp.float32),
        ],
    )
    return pl.pallas_call(
        functools.partial(attention_kernel, first=first, last=last),
        grid_spec=grid_spec,
        out_shape=out_shape,
        compiler_params=pltpu.CompilerParams(
            dimension_semantics=("arbitrary", "arbitrary")
        ),
    )(*operands)


def phase_windows(windows, local_tiles, start, size, tile_count):
    safe = jnp.clip(windows, 0, tile_count - 1)
    position = safe % local_tiles
    inside = (windows >= 0) & (position >= start) & (position < start + size)
    block = (safe // local_tiles) * size + jnp.clip(position - start, 0, size - 1)
    order = jnp.argsort(jnp.logical_not(inside).astype(jnp.int32), axis=1, stable=True)
    ids = jnp.take_along_axis(block, order, axis=1)
    counts = jnp.sum(inside.astype(jnp.int32), axis=1)
    last = jnp.take_along_axis(ids, jnp.maximum(counts - 1, 0)[:, None], axis=1)
    slot = lax.broadcasted_iota(jnp.int32, ids.shape, 1)
    ids = jnp.where(slot < counts[:, None], ids, last)
    ids = jnp.clip(ids, 0, (tile_count // local_tiles) * size - 1)
    return ids.reshape(-1).astype(jnp.int32), counts.astype(jnp.int32)


def phase_bound(local_tiles, tile_count, start, size):
    per_frame = FRAME_ROWS * FRAME_COLS
    frames = tile_count // per_frame
    best = 0
    for i in range(tile_count):
        fi, ri, ci = i // per_frame, i // FRAME_COLS % FRAME_ROWS, i % FRAME_COLS
        total = 0
        for fj in (fi - 1, fi, fi + 1):
            if not 0 <= fj < frames:
                continue
            near = 0
            for j in range(fj * per_frame, (fj + 1) * per_frame):
                rj, cj = j // FRAME_COLS % FRAME_ROWS, j % FRAME_COLS
                if abs(ri - rj) <= 2 and abs(ci - cj) <= 2 and start <= j % local_tiles < start + size:
                    near += 1
            total += min(FRAME_SLOTS, near)
        best = max(best, total)
    return max(1, min(WINDOW_SLOTS, best))


def phase_sizes(local_tiles):
    if local_tiles >= 3:
        return [1, 2] + [1] * (local_tiles - 3)
    return [local_tiles]


def on_device(query_states, key_states, value_states, query_gain, key_gain, windows, tok_count):
    rows = query_states.shape[0]
    local_tiles = rows // TILE_TOKENS
    tile_count = tok_count * local_tiles
    sizes = phase_sizes(local_tiles)
    query_total, key_total = lax.psum((square_sums(query_states), square_sums(key_states)), "head")
    query_normed = normalize_rows(query_states, query_total, query_gain)
    sent_keys = normalize_rows(key_states, key_total, key_gain)
    query_t = query_normed.T
    state = None
    start = 0
    for number, size in enumerate(sizes):
        part = slice(start * TILE_TOKENS, (start + size) * TILE_TOKENS)
        paired = jnp.stack([sent_keys[part], value_states[part]])
        extended = lax.all_gather(paired, "tok", axis=1, tiled=True)
        ids, counts = phase_windows(windows, local_tiles, start, size, tile_count)
        bound = phase_bound(local_tiles, tile_count, start, size)
        state = window_attention(
            query_t, extended, ids, counts, state, number == len(sizes) - 1, bound
        )
        start += size
    return state


def solution(mesh):
    in_specs = (
        P("tok", "head"),
        P("tok", "head"),
        P("tok", "head"),
        P("head"),
        P("head"),
        P("tok", None),
    )
    out_specs = P("tok", "head")
    return jax.shard_map(
        functools.partial(on_device, tok_count=mesh.shape["tok"]),
        mesh=mesh,
        in_specs=in_specs,
        out_specs=out_specs,
        check_vma=False,
    )
```

```python
import functools
import math

import jax
import jax.numpy as jnp
from jax import lax
from jax.experimental import pallas as pl
from jax.experimental.pallas import tpu as pltpu
from jax.sharding import PartitionSpec as P

HEAD_DIM = 128
MODEL_DIM = 3072
TILE_TOKENS = 256
WINDOW_SLOTS = 27
FRAME_SLOTS = 9
FRAME_ROWS = 4
FRAME_COLS = 4
SLOTS_PER_STEP = 1
STATS_HALF = 64


def square_sums(source):
    widened = source.astype(jnp.float32)
    return jnp.sum(widened * widened, axis=1)


def normalize_rows(source, totals, scale_gain):
    widened = source.astype(jnp.float32)
    return (widened * lax.rsqrt(totals[:, None] / MODEL_DIM + 1e-06) * scale_gain).astype(
        jnp.bfloat16
    )


def compact_windows(windows, tile_count):
    valid = windows >= 0
    order = jnp.argsort(jnp.logical_not(valid).astype(jnp.int32), axis=1, stable=True)
    ids = jnp.take_along_axis(windows, order, axis=1)
    counts = jnp.sum(valid.astype(jnp.int32), axis=1)
    last = jnp.take_along_axis(ids, jnp.maximum(counts - 1, 0)[:, None], axis=1)
    slot = lax.broadcasted_iota(jnp.int32, ids.shape, 1)
    ids = jnp.where(slot < counts[:, None], ids, last)
    ids = jnp.clip(ids, 0, tile_count - 1)
    return ids.reshape(-1).astype(jnp.int32), counts.astype(jnp.int32)


def attention_kernel(ids_ref, cnt_ref, q_ref, *refs, first, last):
    k_refs = refs[:SLOTS_PER_STEP]
    v_refs = refs[SLOTS_PER_STEP:2 * SLOTS_PER_STEP]
    rest = refs[2 * SLOTS_PER_STEP:]
    if not first:
        acc_in, stats_in = rest[:2]
        rest = rest[2:]
    if last:
        o_ref = rest[0]
        rest = rest[1:]
    else:
        acc_out, stats_out = rest[:2]
        rest = rest[2:]
    m_sc, l_sc, acc_sc = rest
    t = pl.program_id(0)
    j = pl.program_id(1)
    heads = q_ref.shape[0] // HEAD_DIM
    score_scale = 1.0 / math.sqrt(HEAD_DIM)

    @pl.when(j == 0)
    def _init():
        if first:
            m_sc[...] = jnp.full(m_sc.shape, -jnp.inf, jnp.float32)
            l_sc[...] = jnp.zeros(l_sc.shape, jnp.float32)
            acc_sc[...] = jnp.zeros(acc_sc.shape, jnp.float32)
        else:
            m_sc[...] = stats_in[0, 0]
            l_sc[...] = stats_in[0, 1]
            acc_sc[...] = acc_in[0]

    for sub in range(SLOTS_PER_STEP):
        k_ref = k_refs[sub]
        v_ref = v_refs[sub]

        @pl.when(j * SLOTS_PER_STEP + sub < cnt_ref[t])
        def _step():
            for h in range(heads):
                cols = slice(h * HEAD_DIM, (h + 1) * HEAD_DIM)
                q_t = q_ref[cols, :]
                k = k_ref[0, :, cols]
                v = v_ref[0, :, cols]
                scores = (
                    lax.dot_general(
                        k, q_t, (((1,), (0,)), ((), ())), preferred_element_type=jnp.float32
                    )
                    * score_scale
                )
                m_prev = m_sc[h]
                m_cur = jnp.max(scores, axis=0, keepdims=True)
                m_new = jnp.maximum(m_prev, m_cur)
                alpha = jnp.exp(m_prev - m_new)
                weights = jnp.exp(scores - m_new)
                l_sc[h] = alpha * l_sc[h] + jnp.sum(weights, axis=0, keepdims=True)
                m_sc[h] = m_new
                mixed = lax.dot_general(
                    v, weights.astype(jnp.bfloat16), (((0,), (0,)), ((), ())),
                    preferred_element_type=jnp.float32,
                )
                acc_sc[cols, :] = acc_sc[cols, :] * alpha + mixed

    @pl.when(j == pl.num_programs(1) - 1)
    def _finish():
        if last:
            for h in range(heads):
                cols = slice(h * HEAD_DIM, (h + 1) * HEAD_DIM)
                o_ref[:, cols] = (acc_sc[cols, :] / l_sc[h]).T.astype(o_ref.dtype)
        else:
            acc_out[0] = acc_sc[...]
            stats_out[0, 0] = m_sc[...]
            stats_out[0, 1] = l_sc[...]


def window_attention(query_t, paired, ids, counts, state, last, bound):
    width, rows = query_t.shape
    local_tiles = rows // TILE_TOKENS
    heads = width // HEAD_DIM
    steps = bound // SLOTS_PER_STEP
    first = state is None

    def window_spec(lead, sub):
        return pl.BlockSpec(
            (1, TILE_TOKENS, width),
            lambda t, j, ids, cnt: (lead, ids[t * WINDOW_SLOTS + j * SLOTS_PER_STEP + sub], 0),
        )

    acc_spec = pl.BlockSpec((1, width, TILE_TOKENS), lambda t, j, ids, cnt: (t, 0, 0))
    stats_spec = pl.BlockSpec(
        (1, 2, heads, 1, TILE_TOKENS), lambda t, j, ids, cnt: (t, 0, 0, 0, 0)
    )
    in_specs = [pl.BlockSpec((width, TILE_TOKENS), lambda t, j, ids, cnt: (0, t))]
    in_specs += [window_spec(0, sub) for sub in range(SLOTS_PER_STEP)]
    in_specs += [window_spec(1, sub) for sub in range(SLOTS_PER_STEP)]
    operands = [ids, counts, query_t] + [paired] * (2 * SLOTS_PER_STEP)
    if not first:
        in_specs += [acc_spec, stats_spec]
        operands += list(state)
    if last:
        out_specs = pl.BlockSpec((TILE_TOKENS, width), lambda t, j, ids, cnt: (t, 0))
        out_shape = jax.ShapeDtypeStruct((rows, width), jnp.bfloat16)
    else:
        out_specs = [acc_spec, stats_spec]
        out_shape = [
            jax.ShapeDtypeStruct((local_tiles, width, TILE_TOKENS), jnp.float32),
            jax.ShapeDtypeStruct((local_tiles, 2, heads, 1, TILE_TOKENS), jnp.float32),
        ]
    grid_spec = pltpu.PrefetchScalarGridSpec(
        num_scalar_prefetch=2,
        grid=(local_tiles, steps),
        in_specs=in_specs,
        out_specs=out_specs,
        scratch_shapes=[
            pltpu.VMEM((heads, 1, TILE_TOKENS), jnp.float32),
            pltpu.VMEM((heads, 1, TILE_TOKENS), jnp.float32),
            pltpu.VMEM((width, TILE_TOKENS), jnp.float32),
        ],
    )
    return pl.pallas_call(
        functools.partial(attention_kernel, first=first, last=last),
        grid_spec=grid_spec,
        out_shape=out_shape,
        compiler_params=pltpu.CompilerParams(
            dimension_semantics=("arbitrary", "arbitrary")
        ),
    )(*operands)


def phase_windows(windows, local_tiles, start, size, tile_count):
    safe = jnp.clip(windows, 0, tile_count - 1)
    position = safe % local_tiles
    inside = (windows >= 0) & (position >= start) & (position < start + size)
    block = (safe // local_tiles) * size + jnp.clip(position - start, 0, size - 1)
    order = jnp.argsort(jnp.logical_not(inside).astype(jnp.int32), axis=1, stable=True)
    ids = jnp.take_along_axis(block, order, axis=1)
    counts = jnp.sum(inside.astype(jnp.int32), axis=1)
    last = jnp.take_along_axis(ids, jnp.maximum(counts - 1, 0)[:, None], axis=1)
    slot = lax.broadcasted_iota(jnp.int32, ids.shape, 1)
    ids = jnp.where(slot < counts[:, None], ids, last)
    ids = jnp.clip(ids, 0, (tile_count // local_tiles) * size - 1)
    return ids.reshape(-1).astype(jnp.int32), counts.astype(jnp.int32)


def phase_bound(local_tiles, tile_count, start, size):
    per_frame = FRAME_ROWS * FRAME_COLS
    frames = tile_count // per_frame
    best = 0
    for i in range(tile_count):
        fi, ri, ci = i // per_frame, i // FRAME_COLS % FRAME_ROWS, i % FRAME_COLS
        total = 0
        for fj in (fi - 1, fi, fi + 1):
            if not 0 <= fj < frames:
                continue
            near = 0
            for j in range(fj * per_frame, (fj + 1) * per_frame):
                rj, cj = j // FRAME_COLS % FRAME_ROWS, j % FRAME_COLS
                if abs(ri - rj) <= 2 and abs(ci - cj) <= 2 and start <= j % local_tiles < start + size:
                    near += 1
            total += min(FRAME_SLOTS, near)
        best = max(best, total)
    return max(1, min(WINDOW_SLOTS, best))


def phase_sizes(local_tiles):
    if local_tiles >= 3:
        return [1, 2] + [1] * (local_tiles - 3)
    return [local_tiles]


def head_sums(partial, head_count):
    if head_count & (head_count - 1):
        return lax.psum(partial, "head")
    step = 1
    while step < head_count:
        pairs = [(i, i ^ step) for i in range(head_count)]
        partial = partial + lax.ppermute(partial, "head", pairs)
        step *= 2
    return partial


def on_device(query_states, key_states, value_states, query_gain, key_gain, windows, tok_count, head_count):
    rows = query_states.shape[0]
    local_tiles = rows // TILE_TOKENS
    tile_count = tok_count * local_tiles
    sizes = phase_sizes(local_tiles)
    query_total, key_total = head_sums(
        jnp.stack([square_sums(query_states), square_sums(key_states)]), head_count
    )
    query_normed = normalize_rows(query_states, query_total, query_gain)
    sent_keys = normalize_rows(key_states, key_total, key_gain)
    query_t = query_normed.T
    state = None
    start = 0
    for number, size in enumerate(sizes):
        part = slice(start * TILE_TOKENS, (start + size) * TILE_TOKENS)
        paired = jnp.stack([sent_keys[part], value_states[part]])
        extended = lax.all_gather(paired, "tok", axis=1, tiled=True)
        ids, counts = phase_windows(windows, local_tiles, start, size, tile_count)
        bound = phase_bound(local_tiles, tile_count, start, size)
        state = window_attention(
            query_t, extended, ids, counts, state, number == len(sizes) - 1, bound
        )
        start += size
    return state


def solution(mesh):
    in_specs = (
        P("tok", "head"),
        P("tok", "head"),
        P("tok", "head"),
        P("head"),
        P("head"),
        P("tok", None),
    )
    out_specs = P("tok", "head")
    return jax.shard_map(
        functools.partial(
            on_device, tok_count=mesh.shape["tok"], head_count=mesh.shape["head"]
        ),
        mesh=mesh,
        in_specs=in_specs,
        out_specs=out_specs,
        check_vma=False,
    )
```

```python
import functools
import math

import jax
import jax.numpy as jnp
from jax import lax
from jax.experimental import pallas as pl
from jax.experimental.pallas import tpu as pltpu
from jax.sharding import PartitionSpec as P

HEAD_DIM = 128
MODEL_DIM = 3072
TILE_TOKENS = 256
WINDOW_SLOTS = 27
LOG2_E = 1.4426950408889634
FRAME_SLOTS = 9
FRAME_ROWS = 4
FRAME_COLS = 4
SLOTS_PER_STEP = 1
STATS_HALF = 64


def square_sums(source):
    widened = source.astype(jnp.float32)
    return jnp.sum(widened * widened, axis=1)


def normalize_rows(source, totals, scale_gain):
    widened = source.astype(jnp.float32)
    return (widened * lax.rsqrt(totals[:, None] / MODEL_DIM + 1e-06) * scale_gain).astype(
        jnp.bfloat16
    )


def compact_windows(windows, tile_count):
    valid = windows >= 0
    order = jnp.argsort(jnp.logical_not(valid).astype(jnp.int32), axis=1, stable=True)
    ids = jnp.take_along_axis(windows, order, axis=1)
    counts = jnp.sum(valid.astype(jnp.int32), axis=1)
    last = jnp.take_along_axis(ids, jnp.maximum(counts - 1, 0)[:, None], axis=1)
    slot = lax.broadcasted_iota(jnp.int32, ids.shape, 1)
    ids = jnp.where(slot < counts[:, None], ids, last)
    ids = jnp.clip(ids, 0, tile_count - 1)
    return ids.reshape(-1).astype(jnp.int32), counts.astype(jnp.int32)


def attention_kernel(ids_ref, cnt_ref, q_ref, *refs, first, last):
    k_refs = refs[:SLOTS_PER_STEP]
    v_refs = refs[SLOTS_PER_STEP:2 * SLOTS_PER_STEP]
    rest = refs[2 * SLOTS_PER_STEP:]
    if not first:
        acc_in, stats_in = rest[:2]
        rest = rest[2:]
    if last:
        o_ref = rest[0]
        rest = rest[1:]
    else:
        acc_out, stats_out = rest[:2]
        rest = rest[2:]
    m_sc, l_sc, acc_sc = rest
    t = pl.program_id(0)
    j = pl.program_id(1)
    heads = q_ref.shape[0] // HEAD_DIM
    score_scale = 1.0 / math.sqrt(HEAD_DIM)

    @pl.when(j == 0)
    def _init():
        if first:
            m_sc[...] = jnp.full(m_sc.shape, -jnp.inf, jnp.float32)
            l_sc[...] = jnp.zeros(l_sc.shape, jnp.float32)
            acc_sc[...] = jnp.zeros(acc_sc.shape, jnp.float32)
        else:
            m_sc[...] = stats_in[0, 0]
            l_sc[...] = stats_in[0, 1]
            acc_sc[...] = acc_in[0]

    for sub in range(SLOTS_PER_STEP):
        k_ref = k_refs[sub]
        v_ref = v_refs[sub]

        @pl.when(j * SLOTS_PER_STEP + sub < cnt_ref[t])
        def _step():
            for h in range(heads):
                cols = slice(h * HEAD_DIM, (h + 1) * HEAD_DIM)
                q_t = q_ref[cols, :]
                k = k_ref[0, :, cols]
                v = v_ref[0, :, cols]
                scores = (
                    lax.dot_general(
                        k, q_t, (((1,), (0,)), ((), ())), preferred_element_type=jnp.float32
                    )
                    * (score_scale * LOG2_E)
                )
                m_prev = m_sc[h]
                m_cur = jnp.max(scores, axis=0, keepdims=True)
                m_new = jnp.maximum(m_prev, m_cur)
                alpha = jnp.exp2(m_prev - m_new)
                weights = jnp.exp2(scores - m_new)
                l_sc[h] = alpha * l_sc[h] + jnp.sum(weights, axis=0, keepdims=True)
                m_sc[h] = m_new
                mixed = lax.dot_general(
                    v, weights.astype(jnp.bfloat16), (((0,), (0,)), ((), ())),
                    preferred_element_type=jnp.float32,
                )
                acc_sc[cols, :] = acc_sc[cols, :] * alpha + mixed

    @pl.when(j == pl.num_programs(1) - 1)
    def _finish():
        if last:
            for h in range(heads):
                cols = slice(h * HEAD_DIM, (h + 1) * HEAD_DIM)
                o_ref[:, cols] = (acc_sc[cols, :] / l_sc[h]).T.astype(o_ref.dtype)
        else:
            acc_out[0] = acc_sc[...]
            stats_out[0, 0] = m_sc[...]
            stats_out[0, 1] = l_sc[...]


def window_attention(query_t, paired, ids, counts, state, last, bound):
    width, rows = query_t.shape
    local_tiles = rows // TILE_TOKENS
    heads = width // HEAD_DIM
    steps = bound // SLOTS_PER_STEP
    first = state is None

    def window_spec(lead, sub):
        return pl.BlockSpec(
            (1, TILE_TOKENS, width),
            lambda t, j, ids, cnt: (lead, ids[t * WINDOW_SLOTS + j * SLOTS_PER_STEP + sub], 0),
        )

    acc_spec = pl.BlockSpec((1, width, TILE_TOKENS), lambda t, j, ids, cnt: (t, 0, 0))
    stats_spec = pl.BlockSpec(
        (1, 2, heads, 1, TILE_TOKENS), lambda t, j, ids, cnt: (t, 0, 0, 0, 0)
    )
    in_specs = [pl.BlockSpec((width, TILE_TOKENS), lambda t, j, ids, cnt: (0, t))]
    in_specs += [window_spec(0, sub) for sub in range(SLOTS_PER_STEP)]
    in_specs += [window_spec(1, sub) for sub in range(SLOTS_PER_STEP)]
    operands = [ids, counts, query_t] + [paired] * (2 * SLOTS_PER_STEP)
    if not first:
        in_specs += [acc_spec, stats_spec]
        operands += list(state)
    if last:
        out_specs = pl.BlockSpec((TILE_TOKENS, width), lambda t, j, ids, cnt: (t, 0))
        out_shape = jax.ShapeDtypeStruct((rows, width), jnp.bfloat16)
    else:
        out_specs = [acc_spec, stats_spec]
        out_shape = [
            jax.ShapeDtypeStruct((local_tiles, width, TILE_TOKENS), jnp.float32),
            jax.ShapeDtypeStruct((local_tiles, 2, heads, 1, TILE_TOKENS), jnp.float32),
        ]
    grid_spec = pltpu.PrefetchScalarGridSpec(
        num_scalar_prefetch=2,
        grid=(local_tiles, steps),
        in_specs=in_specs,
        out_specs=out_specs,
        scratch_shapes=[
            pltpu.VMEM((heads, 1, TILE_TOKENS), jnp.float32),
            pltpu.VMEM((heads, 1, TILE_TOKENS), jnp.float32),
            pltpu.VMEM((width, TILE_TOKENS), jnp.float32),
        ],
    )
    return pl.pallas_call(
        functools.partial(attention_kernel, first=first, last=last),
        grid_spec=grid_spec,
        out_shape=out_shape,
        compiler_params=pltpu.CompilerParams(
            dimension_semantics=("arbitrary", "arbitrary")
        ),
    )(*operands)


def phase_windows(windows, local_tiles, start, size, tile_count):
    safe = jnp.clip(windows, 0, tile_count - 1)
    position = safe % local_tiles
    inside = (windows >= 0) & (position >= start) & (position < start + size)
    block = (safe // local_tiles) * size + jnp.clip(position - start, 0, size - 1)
    order = jnp.argsort(jnp.logical_not(inside).astype(jnp.int32), axis=1, stable=True)
    ids = jnp.take_along_axis(block, order, axis=1)
    counts = jnp.sum(inside.astype(jnp.int32), axis=1)
    last = jnp.take_along_axis(ids, jnp.maximum(counts - 1, 0)[:, None], axis=1)
    slot = lax.broadcasted_iota(jnp.int32, ids.shape, 1)
    ids = jnp.where(slot < counts[:, None], ids, last)
    ids = jnp.clip(ids, 0, (tile_count // local_tiles) * size - 1)
    return ids.reshape(-1).astype(jnp.int32), counts.astype(jnp.int32)


def phase_bound(local_tiles, tile_count, start, size):
    per_frame = FRAME_ROWS * FRAME_COLS
    frames = tile_count // per_frame
    best = 0
    for i in range(tile_count):
        fi, ri, ci = i // per_frame, i // FRAME_COLS % FRAME_ROWS, i % FRAME_COLS
        total = 0
        for fj in (fi - 1, fi, fi + 1):
            if not 0 <= fj < frames:
                continue
            near = 0
            for j in range(fj * per_frame, (fj + 1) * per_frame):
                rj, cj = j // FRAME_COLS % FRAME_ROWS, j % FRAME_COLS
                if abs(ri - rj) <= 2 and abs(ci - cj) <= 2 and start <= j % local_tiles < start + size:
                    near += 1
            total += min(FRAME_SLOTS, near)
        best = max(best, total)
    return max(1, min(WINDOW_SLOTS, best))


def phase_sizes(local_tiles):
    if local_tiles >= 3:
        return [1, 2] + [1] * (local_tiles - 3)
    return [local_tiles]


def head_sums(partial, head_count):
    if head_count & (head_count - 1):
        return lax.psum(partial, "head")
    step = 1
    while step < head_count:
        pairs = [(i, i ^ step) for i in range(head_count)]
        partial = partial + lax.ppermute(partial, "head", pairs)
        step *= 2
    return partial


def on_device(query_states, key_states, value_states, query_gain, key_gain, windows, tok_count, head_count):
    rows = query_states.shape[0]
    local_tiles = rows // TILE_TOKENS
    tile_count = tok_count * local_tiles
    sizes = phase_sizes(local_tiles)
    query_total, key_total = head_sums(
        jnp.stack([square_sums(query_states), square_sums(key_states)]), head_count
    )
    query_normed = normalize_rows(query_states, query_total, query_gain)
    sent_keys = normalize_rows(key_states, key_total, key_gain)
    query_t = query_normed.T
    state = None
    start = 0
    for number, size in enumerate(sizes):
        part = slice(start * TILE_TOKENS, (start + size) * TILE_TOKENS)
        paired = jnp.stack([sent_keys[part], value_states[part]])
        extended = lax.all_gather(paired, "tok", axis=1, tiled=True)
        ids, counts = phase_windows(windows, local_tiles, start, size, tile_count)
        bound = phase_bound(local_tiles, tile_count, start, size)
        state = window_attention(
            query_t, extended, ids, counts, state, number == len(sizes) - 1, bound
        )
        start += size
    return state


def solution(mesh):
    in_specs = (
        P("tok", "head"),
        P("tok", "head"),
        P("tok", "head"),
        P("head"),
        P("head"),
        P("tok", None),
    )
    out_specs = P("tok", "head")
    return jax.shard_map(
        functools.partial(
            on_device, tok_count=mesh.shape["tok"], head_count=mesh.shape["head"]
        ),
        mesh=mesh,
        in_specs=in_specs,
        out_specs=out_specs,
        check_vma=False,
    )
```

```python
import functools
import math

import jax
import jax.numpy as jnp
from jax import lax
from jax.experimental import pallas as pl
from jax.experimental.pallas import tpu as pltpu
from jax.sharding import PartitionSpec as P

HEAD_DIM = 128
MODEL_DIM = 3072
TILE_TOKENS = 256
WINDOW_SLOTS = 27
FRAME_SLOTS = 9
FRAME_ROWS = 4
FRAME_COLS = 4
SLOTS_PER_STEP = 1
STATS_HALF = 64


def square_sums(source):
    widened = source.astype(jnp.float32)
    return jnp.sum(widened * widened, axis=1)


def normalize_rows(source, totals, scale_gain):
    widened = source.astype(jnp.float32)
    return (widened * lax.rsqrt(totals[:, None] / MODEL_DIM + 1e-06) * scale_gain).astype(
        jnp.bfloat16
    )


def compact_windows(windows, tile_count):
    valid = windows >= 0
    order = jnp.argsort(jnp.logical_not(valid).astype(jnp.int32), axis=1, stable=True)
    ids = jnp.take_along_axis(windows, order, axis=1)
    counts = jnp.sum(valid.astype(jnp.int32), axis=1)
    last = jnp.take_along_axis(ids, jnp.maximum(counts - 1, 0)[:, None], axis=1)
    slot = lax.broadcasted_iota(jnp.int32, ids.shape, 1)
    ids = jnp.where(slot < counts[:, None], ids, last)
    ids = jnp.clip(ids, 0, tile_count - 1)
    return ids.reshape(-1).astype(jnp.int32), counts.astype(jnp.int32)


def attention_kernel(ids_ref, cnt_ref, q_ref, *refs, first, last):
    k_refs = refs[:SLOTS_PER_STEP]
    v_refs = refs[SLOTS_PER_STEP:2 * SLOTS_PER_STEP]
    rest = refs[2 * SLOTS_PER_STEP:]
    if not first:
        acc_in, stats_in = rest[:2]
        rest = rest[2:]
    if last:
        o_ref = rest[0]
        rest = rest[1:]
    else:
        acc_out, stats_out = rest[:2]
        rest = rest[2:]
    m_sc, l_sc, acc_sc = rest
    t = pl.program_id(0)
    j = pl.program_id(1)
    heads = q_ref.shape[0] // HEAD_DIM
    score_scale = 1.0 / math.sqrt(HEAD_DIM)

    @pl.when(j == 0)
    def _init():
        if first:
            m_sc[...] = jnp.full(m_sc.shape, -jnp.inf, jnp.float32)
            l_sc[...] = jnp.zeros(l_sc.shape, jnp.float32)
            acc_sc[...] = jnp.zeros(acc_sc.shape, jnp.float32)
        else:
            m_sc[...] = stats_in[0, 0]
            l_sc[...] = stats_in[0, 1]
            acc_sc[...] = acc_in[0]

    for sub in range(SLOTS_PER_STEP):
        k_ref = k_refs[sub]
        v_ref = v_refs[sub]

        @pl.when(j * SLOTS_PER_STEP + sub < cnt_ref[t])
        def _step():
            for h in range(heads):
                cols = slice(h * HEAD_DIM, (h + 1) * HEAD_DIM)
                q_t = q_ref[cols, :]
                k = k_ref[0, :, cols]
                v = v_ref[0, :, cols]
                scores = (
                    lax.dot_general(
                        k, q_t, (((1,), (0,)), ((), ())), preferred_element_type=jnp.float32
                    )
                    * score_scale
                )
                m_prev = m_sc[h]
                m_cur = jnp.max(scores, axis=0, keepdims=True)
                m_new = jnp.maximum(m_prev, m_cur)
                alpha = jnp.exp(m_prev - m_new)
                weights = jnp.exp(scores - m_new)
                l_sc[h] = alpha * l_sc[h] + jnp.sum(weights, axis=0, keepdims=True)
                m_sc[h] = m_new
                mixed = lax.dot_general(
                    v, weights.astype(jnp.bfloat16), (((0,), (0,)), ((), ())),
                    preferred_element_type=jnp.float32,
                )
                acc_sc[cols, :] = acc_sc[cols, :] * alpha + mixed

    @pl.when(j == pl.num_programs(1) - 1)
    def _finish():
        if last:
            for h in range(heads):
                cols = slice(h * HEAD_DIM, (h + 1) * HEAD_DIM)
                o_ref[:, cols] = (acc_sc[cols, :] / l_sc[h]).T.astype(o_ref.dtype)
        else:
            acc_out[0] = acc_sc[...]
            stats_out[0, 0] = m_sc[...]
            stats_out[0, 1] = l_sc[...]


def window_attention(query_t, paired, ids, counts, state, last, bound):
    width, rows = query_t.shape
    local_tiles = rows // TILE_TOKENS
    heads = width // HEAD_DIM
    steps = bound // SLOTS_PER_STEP
    first = state is None

    def window_spec(lead, sub):
        return pl.BlockSpec(
            (1, TILE_TOKENS, width),
            lambda t, j, ids, cnt: (lead, ids[t * WINDOW_SLOTS + j * SLOTS_PER_STEP + sub], 0),
        )

    acc_spec = pl.BlockSpec((1, width, TILE_TOKENS), lambda t, j, ids, cnt: (t, 0, 0))
    stats_spec = pl.BlockSpec(
        (1, 2, heads, 1, TILE_TOKENS), lambda t, j, ids, cnt: (t, 0, 0, 0, 0)
    )
    in_specs = [pl.BlockSpec((width, TILE_TOKENS), lambda t, j, ids, cnt: (0, t))]
    in_specs += [window_spec(0, sub) for sub in range(SLOTS_PER_STEP)]
    in_specs += [window_spec(1, sub) for sub in range(SLOTS_PER_STEP)]
    operands = [ids, counts, query_t] + [paired] * (2 * SLOTS_PER_STEP)
    if not first:
        in_specs += [acc_spec, stats_spec]
        operands += list(state)
    if last:
        out_specs = pl.BlockSpec((TILE_TOKENS, width), lambda t, j, ids, cnt: (t, 0))
        out_shape = jax.ShapeDtypeStruct((rows, width), jnp.bfloat16)
    else:
        out_specs = [acc_spec, stats_spec]
        out_shape = [
            jax.ShapeDtypeStruct((local_tiles, width, TILE_TOKENS), jnp.float32),
            jax.ShapeDtypeStruct((local_tiles, 2, heads, 1, TILE_TOKENS), jnp.float32),
        ]
    grid_spec = pltpu.PrefetchScalarGridSpec(
        num_scalar_prefetch=2,
        grid=(local_tiles, steps),
        in_specs=in_specs,
        out_specs=out_specs,
        scratch_shapes=[
            pltpu.VMEM((heads, 1, TILE_TOKENS), jnp.float32),
            pltpu.VMEM((heads, 1, TILE_TOKENS), jnp.float32),
            pltpu.VMEM((width, TILE_TOKENS), jnp.float32),
        ],
    )
    return pl.pallas_call(
        functools.partial(attention_kernel, first=first, last=last),
        grid_spec=grid_spec,
        out_shape=out_shape,
        compiler_params=pltpu.CompilerParams(
            dimension_semantics=("arbitrary", "arbitrary")
        ),
    )(*operands)


def phase_windows(windows, local_tiles, start, size, tile_count, shard, local):
    safe = jnp.clip(windows, 0, tile_count - 1)
    position = safe % local_tiles
    own = safe // local_tiles == shard
    if local:
        inside = (windows >= 0) & own
        block = position
        blocks = local_tiles
    else:
        inside = (windows >= 0) & (position >= start) & (position < start + size) & ~own
        block = (safe // local_tiles) * size + jnp.clip(position - start, 0, size - 1)
        blocks = (tile_count // local_tiles) * size
    order = jnp.argsort(jnp.logical_not(inside).astype(jnp.int32), axis=1, stable=True)
    ids = jnp.take_along_axis(block, order, axis=1)
    counts = jnp.sum(inside.astype(jnp.int32), axis=1)
    last = jnp.take_along_axis(ids, jnp.maximum(counts - 1, 0)[:, None], axis=1)
    slot = lax.broadcasted_iota(jnp.int32, ids.shape, 1)
    ids = jnp.where(slot < counts[:, None], ids, last)
    ids = jnp.clip(ids, 0, blocks - 1)
    return ids.reshape(-1).astype(jnp.int32), counts.astype(jnp.int32)


def phase_bound(local_tiles, tile_count, start, size, local=False):
    per_frame = FRAME_ROWS * FRAME_COLS
    frames = tile_count // per_frame
    best = 0
    for i in range(tile_count):
        fi, ri, ci = i // per_frame, i // FRAME_COLS % FRAME_ROWS, i % FRAME_COLS
        total = 0
        for fj in (fi - 1, fi, fi + 1):
            if not 0 <= fj < frames:
                continue
            near = 0
            for j in range(fj * per_frame, (fj + 1) * per_frame):
                rj, cj = j // FRAME_COLS % FRAME_ROWS, j % FRAME_COLS
                if local:
                    chosen = j // local_tiles == i // local_tiles
                else:
                    chosen = start <= j % local_tiles < start + size
                if abs(ri - rj) <= 2 and abs(ci - cj) <= 2 and chosen:
                    near += 1
            total += min(FRAME_SLOTS, near)
        best = max(best, total)
    return max(1, min(WINDOW_SLOTS, best))


def phase_sizes(local_tiles):
    if local_tiles >= 3:
        return [1, 2] + [1] * (local_tiles - 3)
    return [local_tiles]


def head_sums(partial, head_count):
    if head_count & (head_count - 1):
        return lax.psum(partial, "head")
    step = 1
    while step < head_count:
        pairs = [(i, i ^ step) for i in range(head_count)]
        partial = partial + lax.ppermute(partial, "head", pairs)
        step *= 2
    return partial


def on_device(query_states, key_states, value_states, query_gain, key_gain, windows, tok_count, head_count):
    rows = query_states.shape[0]
    local_tiles = rows // TILE_TOKENS
    tile_count = tok_count * local_tiles
    sizes = phase_sizes(local_tiles)
    query_total, key_total = head_sums(
        jnp.stack([square_sums(query_states), square_sums(key_states)]), head_count
    )
    query_normed = normalize_rows(query_states, query_total, query_gain)
    sent_keys = normalize_rows(key_states, key_total, key_gain)
    query_t = query_normed.T
    shard = lax.axis_index("tok")
    own = jnp.stack([sent_keys, value_states])
    ids, counts = phase_windows(windows, local_tiles, 0, local_tiles, tile_count, shard, True)
    bound = phase_bound(local_tiles, tile_count, 0, local_tiles, local=True)
    state = window_attention(query_t, own, ids, counts, None, False, bound)
    start = 0
    for number, size in enumerate(sizes):
        part = slice(start * TILE_TOKENS, (start + size) * TILE_TOKENS)
        paired = jnp.stack([sent_keys[part], value_states[part]])
        extended = lax.all_gather(paired, "tok", axis=1, tiled=True)
        ids, counts = phase_windows(windows, local_tiles, start, size, tile_count, shard, False)
        bound = phase_bound(local_tiles, tile_count, start, size)
        state = window_attention(
            query_t, extended, ids, counts, state, number == len(sizes) - 1, bound
        )
        start += size
    return state


def solution(mesh):
    in_specs = (
        P("tok", "head"),
        P("tok", "head"),
        P("tok", "head"),
        P("head"),
        P("head"),
        P("tok", None),
    )
    out_specs = P("tok", "head")
    return jax.shard_map(
        functools.partial(
            on_device, tok_count=mesh.shape["tok"], head_count=mesh.shape["head"]
        ),
        mesh=mesh,
        in_specs=in_specs,
        out_specs=out_specs,
        check_vma=False,
    )
```

```python
import functools
import math

import jax
import jax.numpy as jnp
from jax import lax
from jax.experimental import pallas as pl
from jax.experimental.pallas import tpu as pltpu
from jax.sharding import PartitionSpec as P

HEAD_DIM = 128
MODEL_DIM = 3072
TILE_TOKENS = 256
WINDOW_SLOTS = 27
FRAME_SLOTS = 9
FRAME_ROWS = 4
FRAME_COLS = 4
SLOTS_PER_STEP = 1
STATS_HALF = 64


def square_sums(source):
    widened = source.astype(jnp.float32)
    return jnp.sum(widened * widened, axis=1)


def normalize_rows(source, totals, scale_gain):
    widened = source.astype(jnp.float32)
    return (widened * lax.rsqrt(totals[:, None] / MODEL_DIM + 1e-06) * scale_gain).astype(
        jnp.bfloat16
    )


def compact_windows(windows, tile_count):
    valid = windows >= 0
    order = jnp.argsort(jnp.logical_not(valid).astype(jnp.int32), axis=1, stable=True)
    ids = jnp.take_along_axis(windows, order, axis=1)
    counts = jnp.sum(valid.astype(jnp.int32), axis=1)
    last = jnp.take_along_axis(ids, jnp.maximum(counts - 1, 0)[:, None], axis=1)
    slot = lax.broadcasted_iota(jnp.int32, ids.shape, 1)
    ids = jnp.where(slot < counts[:, None], ids, last)
    ids = jnp.clip(ids, 0, tile_count - 1)
    return ids.reshape(-1).astype(jnp.int32), counts.astype(jnp.int32)


def attention_kernel(ids_ref, cnt_ref, q_ref, *refs, first, last):
    k_refs = refs[:SLOTS_PER_STEP]
    v_refs = refs[SLOTS_PER_STEP:2 * SLOTS_PER_STEP]
    rest = refs[2 * SLOTS_PER_STEP:]
    if not first:
        acc_in, stats_in = rest[:2]
        rest = rest[2:]
    if last:
        o_ref = rest[0]
        rest = rest[1:]
    else:
        acc_out, stats_out = rest[:2]
        rest = rest[2:]
    m_sc, l_sc, acc_sc = rest
    t = pl.program_id(0)
    j = pl.program_id(1)
    heads = q_ref.shape[0] // HEAD_DIM
    score_scale = 1.0 / math.sqrt(HEAD_DIM)

    @pl.when(j == 0)
    def _init():
        if first:
            m_sc[...] = jnp.full(m_sc.shape, -jnp.inf, jnp.float32)
            l_sc[...] = jnp.zeros(l_sc.shape, jnp.float32)
            acc_sc[...] = jnp.zeros(acc_sc.shape, jnp.float32)
        else:
            m_sc[...] = stats_in[0, 0]
            l_sc[...] = stats_in[0, 1]
            acc_sc[...] = acc_in[0]

    for sub in range(SLOTS_PER_STEP):
        k_ref = k_refs[sub]
        v_ref = v_refs[sub]

        @pl.when(j * SLOTS_PER_STEP + sub < cnt_ref[t])
        def _step():
            for h in range(heads):
                cols = slice(h * HEAD_DIM, (h + 1) * HEAD_DIM)
                q_t = q_ref[cols, :]
                k = k_ref[0, :, cols]
                v = v_ref[0, :, cols]
                scores = (
                    lax.dot_general(
                        k, q_t, (((1,), (0,)), ((), ())), preferred_element_type=jnp.float32
                    )
                    * score_scale
                )
                m_prev = m_sc[h]
                m_cur = jnp.max(scores, axis=0, keepdims=True)
                m_new = jnp.maximum(m_prev, m_cur)
                alpha = jnp.exp(m_prev - m_new)
                weights = jnp.exp(scores - m_new)
                l_sc[h] = alpha * l_sc[h] + jnp.sum(weights, axis=0, keepdims=True)
                m_sc[h] = m_new
                mixed = lax.dot_general(
                    v, weights.astype(jnp.bfloat16), (((0,), (0,)), ((), ())),
                    preferred_element_type=jnp.float32,
                )
                acc_sc[cols, :] = acc_sc[cols, :] * alpha + mixed

    @pl.when(j == pl.num_programs(1) - 1)
    def _finish():
        if last:
            for h in range(heads):
                cols = slice(h * HEAD_DIM, (h + 1) * HEAD_DIM)
                o_ref[:, cols] = (acc_sc[cols, :] / l_sc[h]).T.astype(o_ref.dtype)
        else:
            acc_out[0] = acc_sc[...]
            stats_out[0, 0] = m_sc[...]
            stats_out[0, 1] = l_sc[...]


def window_attention(query_t, paired, ids, counts, state, last, bound):
    width, rows = query_t.shape
    local_tiles = rows // TILE_TOKENS
    heads = width // HEAD_DIM
    steps = bound // SLOTS_PER_STEP
    first = state is None

    def window_spec(lead, sub):
        return pl.BlockSpec(
            (1, TILE_TOKENS, width),
            lambda t, j, ids, cnt: (lead, ids[t * WINDOW_SLOTS + j * SLOTS_PER_STEP + sub], 0),
        )

    acc_spec = pl.BlockSpec((1, width, TILE_TOKENS), lambda t, j, ids, cnt: (t, 0, 0))
    stats_spec = pl.BlockSpec(
        (1, 2, heads, 1, TILE_TOKENS), lambda t, j, ids, cnt: (t, 0, 0, 0, 0)
    )
    in_specs = [pl.BlockSpec((width, TILE_TOKENS), lambda t, j, ids, cnt: (0, t))]
    in_specs += [window_spec(0, sub) for sub in range(SLOTS_PER_STEP)]
    in_specs += [window_spec(1, sub) for sub in range(SLOTS_PER_STEP)]
    operands = [ids, counts, query_t] + [paired] * (2 * SLOTS_PER_STEP)
    if not first:
        in_specs += [acc_spec, stats_spec]
        operands += list(state)
    if last:
        out_specs = pl.BlockSpec((TILE_TOKENS, width), lambda t, j, ids, cnt: (t, 0))
        out_shape = jax.ShapeDtypeStruct((rows, width), jnp.bfloat16)
    else:
        out_specs = [acc_spec, stats_spec]
        out_shape = [
            jax.ShapeDtypeStruct((local_tiles, width, TILE_TOKENS), jnp.float32),
            jax.ShapeDtypeStruct((local_tiles, 2, heads, 1, TILE_TOKENS), jnp.float32),
        ]
    grid_spec = pltpu.PrefetchScalarGridSpec(
        num_scalar_prefetch=2,
        grid=(local_tiles, steps),
        in_specs=in_specs,
        out_specs=out_specs,
        scratch_shapes=[
            pltpu.VMEM((heads, 1, TILE_TOKENS), jnp.float32),
            pltpu.VMEM((heads, 1, TILE_TOKENS), jnp.float32),
            pltpu.VMEM((width, TILE_TOKENS), jnp.float32),
        ],
    )
    return pl.pallas_call(
        functools.partial(attention_kernel, first=first, last=last),
        grid_spec=grid_spec,
        out_shape=out_shape,
        compiler_params=pltpu.CompilerParams(
            dimension_semantics=("arbitrary", "arbitrary")
        ),
    )(*operands)


def phase_windows(windows, local_tiles, start, size, tile_count, shard, local):
    safe = jnp.clip(windows, 0, tile_count - 1)
    position = safe % local_tiles
    own = safe // local_tiles == shard
    if local:
        inside = (windows >= 0) & own
        block = position
        blocks = local_tiles
    else:
        inside = (windows >= 0) & (position >= start) & (position < start + size) & ~own
        block = (safe // local_tiles) * size + jnp.clip(position - start, 0, size - 1)
        blocks = (tile_count // local_tiles) * size
    order = jnp.argsort(jnp.logical_not(inside).astype(jnp.int32), axis=1, stable=True)
    ids = jnp.take_along_axis(block, order, axis=1)
    counts = jnp.sum(inside.astype(jnp.int32), axis=1)
    last = jnp.take_along_axis(ids, jnp.maximum(counts - 1, 0)[:, None], axis=1)
    slot = lax.broadcasted_iota(jnp.int32, ids.shape, 1)
    ids = jnp.where(slot < counts[:, None], ids, last)
    ids = jnp.clip(ids, 0, blocks - 1)
    return ids.reshape(-1).astype(jnp.int32), counts.astype(jnp.int32)


def phase_bound(local_tiles, tile_count, start, size, local=False):
    per_frame = FRAME_ROWS * FRAME_COLS
    frames = tile_count // per_frame
    best = 0
    for i in range(tile_count):
        fi, ri, ci = i // per_frame, i // FRAME_COLS % FRAME_ROWS, i % FRAME_COLS
        total = 0
        for fj in (fi - 1, fi, fi + 1):
            if not 0 <= fj < frames:
                continue
            near = 0
            for j in range(fj * per_frame, (fj + 1) * per_frame):
                rj, cj = j // FRAME_COLS % FRAME_ROWS, j % FRAME_COLS
                if local:
                    chosen = j // local_tiles == i // local_tiles
                else:
                    chosen = start <= j % local_tiles < start + size
                if abs(ri - rj) <= 2 and abs(ci - cj) <= 2 and chosen:
                    near += 1
            total += min(FRAME_SLOTS, near)
        best = max(best, total)
    return max(1, min(WINDOW_SLOTS, best))


def phase_sizes(local_tiles):
    if local_tiles >= 3:
        return [1, 2] + [1] * (local_tiles - 3)
    return [local_tiles]


def head_sums(partial, head_count):
    if head_count & (head_count - 1):
        return lax.psum(partial, "head")
    step = 1
    while step < head_count:
        pairs = [(i, i ^ step) for i in range(head_count)]
        partial = partial + lax.ppermute(partial, "head", pairs)
        step *= 2
    return partial


def on_device(query_states, key_states, value_states, query_gain, key_gain, windows, tok_count, head_count):
    rows = query_states.shape[0]
    local_tiles = rows // TILE_TOKENS
    tile_count = tok_count * local_tiles
    sizes = phase_sizes(local_tiles)
    key_total = head_sums(square_sums(key_states), head_count)
    sent_keys = normalize_rows(key_states, key_total, key_gain)
    query_in, _ = lax.optimization_barrier((query_states, sent_keys))
    query_total = head_sums(square_sums(query_in), head_count)
    query_normed = normalize_rows(query_in, query_total, query_gain)
    query_t = query_normed.T
    shard = lax.axis_index("tok")
    own = jnp.stack([sent_keys, value_states])
    ids, counts = phase_windows(windows, local_tiles, 0, local_tiles, tile_count, shard, True)
    bound = phase_bound(local_tiles, tile_count, 0, local_tiles, local=True)
    state = window_attention(query_t, own, ids, counts, None, False, bound)
    start = 0
    for number, size in enumerate(sizes):
        part = slice(start * TILE_TOKENS, (start + size) * TILE_TOKENS)
        paired = jnp.stack([sent_keys[part], value_states[part]])
        extended = lax.all_gather(paired, "tok", axis=1, tiled=True)
        ids, counts = phase_windows(windows, local_tiles, start, size, tile_count, shard, False)
        bound = phase_bound(local_tiles, tile_count, start, size)
        state = window_attention(
            query_t, extended, ids, counts, state, number == len(sizes) - 1, bound
        )
        start += size
    return state


def solution(mesh):
    in_specs = (
        P("tok", "head"),
        P("tok", "head"),
        P("tok", "head"),
        P("head"),
        P("head"),
        P("tok", None),
    )
    out_specs = P("tok", "head")
    return jax.shard_map(
        functools.partial(
            on_device, tok_count=mesh.shape["tok"], head_count=mesh.shape["head"]
        ),
        mesh=mesh,
        in_specs=in_specs,
        out_specs=out_specs,
        check_vma=False,
    )
```

```python
import functools
import math

import jax
import jax.numpy as jnp
from jax import lax
from jax.experimental import pallas as pl
from jax.experimental.pallas import tpu as pltpu
from jax.sharding import PartitionSpec as P

HEAD_DIM = 128
MODEL_DIM = 3072
TILE_TOKENS = 256
WINDOW_SLOTS = 27
LOG2_E = 1.4426950408889634
FRAME_SLOTS = 9
FRAME_ROWS = 4
FRAME_COLS = 4
SLOTS_PER_STEP = 1
STATS_HALF = 64


def square_sums(source):
    widened = source.astype(jnp.float32)
    return jnp.sum(widened * widened, axis=1)


def normalize_rows(source, totals, scale_gain):
    widened = source.astype(jnp.float32)
    return (widened * lax.rsqrt(totals[:, None] / MODEL_DIM + 1e-06) * scale_gain).astype(
        jnp.bfloat16
    )


def compact_windows(windows, tile_count):
    valid = windows >= 0
    order = jnp.argsort(jnp.logical_not(valid).astype(jnp.int32), axis=1, stable=True)
    ids = jnp.take_along_axis(windows, order, axis=1)
    counts = jnp.sum(valid.astype(jnp.int32), axis=1)
    last = jnp.take_along_axis(ids, jnp.maximum(counts - 1, 0)[:, None], axis=1)
    slot = lax.broadcasted_iota(jnp.int32, ids.shape, 1)
    ids = jnp.where(slot < counts[:, None], ids, last)
    ids = jnp.clip(ids, 0, tile_count - 1)
    return ids.reshape(-1).astype(jnp.int32), counts.astype(jnp.int32)


def attention_kernel(ids_ref, cnt_ref, q_ref, *refs, first, last):
    k_refs = refs[:SLOTS_PER_STEP]
    v_refs = refs[SLOTS_PER_STEP:2 * SLOTS_PER_STEP]
    rest = refs[2 * SLOTS_PER_STEP:]
    if not first:
        acc_in, stats_in = rest[:2]
        rest = rest[2:]
    if last:
        o_ref = rest[0]
        rest = rest[1:]
    else:
        acc_out, stats_out = rest[:2]
        rest = rest[2:]
    m_sc, l_sc, acc_sc = rest
    t = pl.program_id(0)
    j = pl.program_id(1)
    heads = q_ref.shape[0] // HEAD_DIM
    score_scale = 1.0 / math.sqrt(HEAD_DIM)

    @pl.when(j == 0)
    def _init():
        if first:
            m_sc[...] = jnp.full(m_sc.shape, -jnp.inf, jnp.float32)
            l_sc[...] = jnp.zeros(l_sc.shape, jnp.float32)
            acc_sc[...] = jnp.zeros(acc_sc.shape, jnp.float32)
        else:
            m_sc[...] = stats_in[0, 0]
            l_sc[...] = stats_in[0, 1]
            acc_sc[...] = acc_in[0]

    for sub in range(SLOTS_PER_STEP):
        k_ref = k_refs[sub]
        v_ref = v_refs[sub]

        @pl.when(j * SLOTS_PER_STEP + sub < cnt_ref[t])
        def _step():
            for h in range(heads):
                cols = slice(h * HEAD_DIM, (h + 1) * HEAD_DIM)
                q_t = q_ref[cols, :]
                k = k_ref[0, :, cols]
                v = v_ref[0, :, cols]
                scores = (
                    lax.dot_general(
                        k, q_t, (((1,), (0,)), ((), ())), preferred_element_type=jnp.float32
                    )
                    * (score_scale * LOG2_E)
                )
                m_prev = m_sc[h]
                m_cur = jnp.max(scores, axis=0, keepdims=True)
                m_new = jnp.maximum(m_prev, m_cur)
                alpha = jnp.exp2(m_prev - m_new)
                weights = jnp.exp2(scores - m_new)
                l_sc[h] = alpha * l_sc[h] + jnp.sum(weights, axis=0, keepdims=True)
                m_sc[h] = m_new
                mixed = lax.dot_general(
                    v, weights.astype(jnp.bfloat16), (((0,), (0,)), ((), ())),
                    preferred_element_type=jnp.float32,
                )
                acc_sc[cols, :] = acc_sc[cols, :] * alpha + mixed

    @pl.when(j == pl.num_programs(1) - 1)
    def _finish():
        if last:
            for h in range(heads):
                cols = slice(h * HEAD_DIM, (h + 1) * HEAD_DIM)
                o_ref[:, cols] = (acc_sc[cols, :] / l_sc[h]).T.astype(o_ref.dtype)
        else:
            acc_out[0] = acc_sc[...]
            stats_out[0, 0] = m_sc[...]
            stats_out[0, 1] = l_sc[...]


def window_attention(query_t, paired, ids, counts, state, last, bound):
    width, rows = query_t.shape
    local_tiles = rows // TILE_TOKENS
    heads = width // HEAD_DIM
    steps = bound // SLOTS_PER_STEP
    first = state is None

    def window_spec(lead, sub):
        return pl.BlockSpec(
            (1, TILE_TOKENS, width),
            lambda t, j, ids, cnt: (lead, ids[t * WINDOW_SLOTS + j * SLOTS_PER_STEP + sub], 0),
        )

    acc_spec = pl.BlockSpec((1, width, TILE_TOKENS), lambda t, j, ids, cnt: (t, 0, 0))
    stats_spec = pl.BlockSpec(
        (1, 2, heads, 1, TILE_TOKENS), lambda t, j, ids, cnt: (t, 0, 0, 0, 0)
    )
    in_specs = [pl.BlockSpec((width, TILE_TOKENS), lambda t, j, ids, cnt: (0, t))]
    in_specs += [window_spec(0, sub) for sub in range(SLOTS_PER_STEP)]
    in_specs += [window_spec(1, sub) for sub in range(SLOTS_PER_STEP)]
    operands = [ids, counts, query_t] + [paired] * (2 * SLOTS_PER_STEP)
    if not first:
        in_specs += [acc_spec, stats_spec]
        operands += list(state)
    if last:
        out_specs = pl.BlockSpec((TILE_TOKENS, width), lambda t, j, ids, cnt: (t, 0))
        out_shape = jax.ShapeDtypeStruct((rows, width), jnp.bfloat16)
    else:
        out_specs = [acc_spec, stats_spec]
        out_shape = [
            jax.ShapeDtypeStruct((local_tiles, width, TILE_TOKENS), jnp.float32),
            jax.ShapeDtypeStruct((local_tiles, 2, heads, 1, TILE_TOKENS), jnp.float32),
        ]
    grid_spec = pltpu.PrefetchScalarGridSpec(
        num_scalar_prefetch=2,
        grid=(local_tiles, steps),
        in_specs=in_specs,
        out_specs=out_specs,
        scratch_shapes=[
            pltpu.VMEM((heads, 1, TILE_TOKENS), jnp.float32),
            pltpu.VMEM((heads, 1, TILE_TOKENS), jnp.float32),
            pltpu.VMEM((width, TILE_TOKENS), jnp.float32),
        ],
    )
    return pl.pallas_call(
        functools.partial(attention_kernel, first=first, last=last),
        grid_spec=grid_spec,
        out_shape=out_shape,
        compiler_params=pltpu.CompilerParams(
            dimension_semantics=("arbitrary", "arbitrary")
        ),
    )(*operands)


def phase_windows(windows, local_tiles, start, size, tile_count, shard, local):
    safe = jnp.clip(windows, 0, tile_count - 1)
    position = safe % local_tiles
    own = safe // local_tiles == shard
    if local:
        inside = (windows >= 0) & own
        block = position
        blocks = local_tiles
    else:
        inside = (windows >= 0) & (position >= start) & (position < start + size) & ~own
        block = (safe // local_tiles) * size + jnp.clip(position - start, 0, size - 1)
        blocks = (tile_count // local_tiles) * size
    order = jnp.argsort(jnp.logical_not(inside).astype(jnp.int32), axis=1, stable=True)
    ids = jnp.take_along_axis(block, order, axis=1)
    counts = jnp.sum(inside.astype(jnp.int32), axis=1)
    last = jnp.take_along_axis(ids, jnp.maximum(counts - 1, 0)[:, None], axis=1)
    slot = lax.broadcasted_iota(jnp.int32, ids.shape, 1)
    ids = jnp.where(slot < counts[:, None], ids, last)
    ids = jnp.clip(ids, 0, blocks - 1)
    return ids.reshape(-1).astype(jnp.int32), counts.astype(jnp.int32)


def phase_bound(local_tiles, tile_count, start, size, local=False):
    per_frame = FRAME_ROWS * FRAME_COLS
    frames = tile_count // per_frame
    best = 0
    for i in range(tile_count):
        fi, ri, ci = i // per_frame, i // FRAME_COLS % FRAME_ROWS, i % FRAME_COLS
        total = 0
        for fj in (fi - 1, fi, fi + 1):
            if not 0 <= fj < frames:
                continue
            near = 0
            for j in range(fj * per_frame, (fj + 1) * per_frame):
                rj, cj = j // FRAME_COLS % FRAME_ROWS, j % FRAME_COLS
                if local:
                    chosen = j // local_tiles == i // local_tiles
                else:
                    chosen = start <= j % local_tiles < start + size
                if abs(ri - rj) <= 2 and abs(ci - cj) <= 2 and chosen:
                    near += 1
            total += min(FRAME_SLOTS, near)
        best = max(best, total)
    return max(1, min(WINDOW_SLOTS, best))


def phase_sizes(local_tiles):
    if local_tiles >= 3:
        return [1, 2] + [1] * (local_tiles - 3)
    return [local_tiles]


def head_sums(partial, head_count):
    if head_count & (head_count - 1):
        return lax.psum(partial, "head")
    step = 1
    while step < head_count:
        pairs = [(i, i ^ step) for i in range(head_count)]
        partial = partial + lax.ppermute(partial, "head", pairs)
        step *= 2
    return partial


def on_device(query_states, key_states, value_states, query_gain, key_gain, windows, tok_count, head_count):
    rows = query_states.shape[0]
    local_tiles = rows // TILE_TOKENS
    tile_count = tok_count * local_tiles
    sizes = phase_sizes(local_tiles)
    key_total = head_sums(square_sums(key_states), head_count)
    sent_keys = normalize_rows(key_states, key_total, key_gain)
    query_in, _ = lax.optimization_barrier((query_states, sent_keys))
    query_total = head_sums(square_sums(query_in), head_count)
    query_normed = normalize_rows(query_in, query_total, query_gain)
    query_t = query_normed.T
    shard = lax.axis_index("tok")
    own = jnp.stack([sent_keys, value_states])
    ids, counts = phase_windows(windows, local_tiles, 0, local_tiles, tile_count, shard, True)
    bound = phase_bound(local_tiles, tile_count, 0, local_tiles, local=True)
    state = window_attention(query_t, own, ids, counts, None, False, bound)
    start = 0
    for number, size in enumerate(sizes):
        part = slice(start * TILE_TOKENS, (start + size) * TILE_TOKENS)
        paired = jnp.stack([sent_keys[part], value_states[part]])
        extended = lax.all_gather(paired, "tok", axis=1, tiled=True)
        ids, counts = phase_windows(windows, local_tiles, start, size, tile_count, shard, False)
        bound = phase_bound(local_tiles, tile_count, start, size)
        state = window_attention(
            query_t, extended, ids, counts, state, number == len(sizes) - 1, bound
        )
        start += size
    return state


def solution(mesh):
    in_specs = (
        P("tok", "head"),
        P("tok", "head"),
        P("tok", "head"),
        P("head"),
        P("head"),
        P("tok", None),
    )
    out_specs = P("tok", "head")
    return jax.shard_map(
        functools.partial(
            on_device, tok_count=mesh.shape["tok"], head_count=mesh.shape["head"]
        ),
        mesh=mesh,
        in_specs=in_specs,
        out_specs=out_specs,
        check_vma=False,
    )
```

```python
import functools
import math

import jax
import jax.numpy as jnp
from jax import lax
from jax.experimental import pallas as pl
from jax.experimental.pallas import tpu as pltpu
from jax.sharding import PartitionSpec as P

HEAD_DIM = 128
MODEL_DIM = 3072
TILE_TOKENS = 256
WINDOW_SLOTS = 27
LOG2_E = 1.4426950408889634
FRAME_SLOTS = 9
FRAME_ROWS = 4
FRAME_COLS = 4
SLOTS_PER_STEP = 1
STATS_HALF = 64


def square_sums(source):
    widened = source.astype(jnp.float32)
    return jnp.sum(widened * widened, axis=1)


def normalize_rows(source, totals, scale_gain):
    widened = source.astype(jnp.float32)
    return (widened * lax.rsqrt(totals[:, None] / MODEL_DIM + 1e-06) * scale_gain).astype(
        jnp.bfloat16
    )


def compact_windows(windows, tile_count):
    valid = windows >= 0
    order = jnp.argsort(jnp.logical_not(valid).astype(jnp.int32), axis=1, stable=True)
    ids = jnp.take_along_axis(windows, order, axis=1)
    counts = jnp.sum(valid.astype(jnp.int32), axis=1)
    last = jnp.take_along_axis(ids, jnp.maximum(counts - 1, 0)[:, None], axis=1)
    slot = lax.broadcasted_iota(jnp.int32, ids.shape, 1)
    ids = jnp.where(slot < counts[:, None], ids, last)
    ids = jnp.clip(ids, 0, tile_count - 1)
    return ids.reshape(-1).astype(jnp.int32), counts.astype(jnp.int32)


def attention_kernel(ids_ref, cnt_ref, q_ref, *refs, first, last):
    k_refs = refs[:SLOTS_PER_STEP]
    v_refs = refs[SLOTS_PER_STEP:2 * SLOTS_PER_STEP]
    rest = refs[2 * SLOTS_PER_STEP:]
    if not first:
        acc_in, stats_in = rest[:2]
        rest = rest[2:]
    if last:
        o_ref = rest[0]
        rest = rest[1:]
    else:
        acc_out, stats_out = rest[:2]
        rest = rest[2:]
    m_sc, l_sc, acc_sc = rest
    t = pl.program_id(0)
    j = pl.program_id(1)
    heads = q_ref.shape[0] // HEAD_DIM
    score_scale = 1.0 / math.sqrt(HEAD_DIM)

    @pl.when(j == 0)
    def _init():
        if first:
            m_sc[...] = jnp.full(m_sc.shape, -jnp.inf, jnp.float32)
            l_sc[...] = jnp.zeros(l_sc.shape, jnp.float32)
            acc_sc[...] = jnp.zeros(acc_sc.shape, jnp.float32)
        else:
            m_sc[...] = stats_in[0, 0]
            l_sc[...] = stats_in[0, 1]
            acc_sc[...] = acc_in[0]

    for sub in range(SLOTS_PER_STEP):
        k_ref = k_refs[sub]
        v_ref = v_refs[sub]

        @pl.when(j * SLOTS_PER_STEP + sub < cnt_ref[t])
        def _step():
            for h in range(heads):
                cols = slice(h * HEAD_DIM, (h + 1) * HEAD_DIM)
                q_t = q_ref[cols, :]
                k = k_ref[0, :, cols]
                v = v_ref[0, :, cols]
                scores = (
                    lax.dot_general(
                        k, q_t, (((1,), (0,)), ((), ())), preferred_element_type=jnp.float32
                    )
                    * (score_scale * LOG2_E)
                )
                m_prev = m_sc[h]
                m_cur = jnp.max(scores, axis=0, keepdims=True)
                m_new = jnp.maximum(m_prev, m_cur)
                alpha = jnp.exp2(m_prev - m_new)
                weights = jnp.exp2(scores - m_new)
                l_sc[h] = alpha * l_sc[h] + jnp.sum(weights, axis=0, keepdims=True)
                m_sc[h] = m_new
                mixed = lax.dot_general(
                    v, weights.astype(jnp.bfloat16), (((0,), (0,)), ((), ())),
                    preferred_element_type=jnp.float32,
                )
                acc_sc[cols, :] = acc_sc[cols, :] * alpha + mixed

    @pl.when(j == pl.num_programs(1) - 1)
    def _finish():
        if last:
            for h in range(heads):
                cols = slice(h * HEAD_DIM, (h + 1) * HEAD_DIM)
                o_ref[:, cols] = (acc_sc[cols, :] / l_sc[h]).T.astype(o_ref.dtype)
        else:
            acc_out[0] = acc_sc[...]
            stats_out[0, 0] = m_sc[...]
            stats_out[0, 1] = l_sc[...]


def window_attention(query_t, paired, ids, counts, state, last, bound):
    width, rows = query_t.shape
    local_tiles = rows // TILE_TOKENS
    heads = width // HEAD_DIM
    steps = bound // SLOTS_PER_STEP
    first = state is None

    def window_spec(lead, sub):
        return pl.BlockSpec(
            (1, TILE_TOKENS, width),
            lambda t, j, ids, cnt: (lead, ids[t * WINDOW_SLOTS + j * SLOTS_PER_STEP + sub], 0),
        )

    acc_spec = pl.BlockSpec((1, width, TILE_TOKENS), lambda t, j, ids, cnt: (t, 0, 0))
    stats_spec = pl.BlockSpec(
        (1, 2, heads, 1, TILE_TOKENS), lambda t, j, ids, cnt: (t, 0, 0, 0, 0)
    )
    in_specs = [pl.BlockSpec((width, TILE_TOKENS), lambda t, j, ids, cnt: (0, t))]
    in_specs += [window_spec(0, sub) for sub in range(SLOTS_PER_STEP)]
    in_specs += [window_spec(1, sub) for sub in range(SLOTS_PER_STEP)]
    operands = [ids, counts, query_t] + [paired] * (2 * SLOTS_PER_STEP)
    if not first:
        in_specs += [acc_spec, stats_spec]
        operands += list(state)
    if last:
        out_specs = pl.BlockSpec((TILE_TOKENS, width), lambda t, j, ids, cnt: (t, 0))
        out_shape = jax.ShapeDtypeStruct((rows, width), jnp.bfloat16)
    else:
        out_specs = [acc_spec, stats_spec]
        out_shape = [
            jax.ShapeDtypeStruct((local_tiles, width, TILE_TOKENS), jnp.float32),
            jax.ShapeDtypeStruct((local_tiles, 2, heads, 1, TILE_TOKENS), jnp.float32),
        ]
    grid_spec = pltpu.PrefetchScalarGridSpec(
        num_scalar_prefetch=2,
        grid=(local_tiles, steps),
        in_specs=in_specs,
        out_specs=out_specs,
        scratch_shapes=[
            pltpu.VMEM((heads, 1, TILE_TOKENS), jnp.float32),
            pltpu.VMEM((heads, 1, TILE_TOKENS), jnp.float32),
            pltpu.VMEM((width, TILE_TOKENS), jnp.float32),
        ],
    )
    return pl.pallas_call(
        functools.partial(attention_kernel, first=first, last=last),
        grid_spec=grid_spec,
        out_shape=out_shape,
        compiler_params=pltpu.CompilerParams(
            dimension_semantics=("arbitrary", "arbitrary")
        ),
    )(*operands)


def phase_windows(windows, local_tiles, start, size, tile_count, shard, local):
    safe = jnp.clip(windows, 0, tile_count - 1)
    position = safe % local_tiles
    own = safe // local_tiles == shard
    if local:
        inside = (windows >= 0) & own
        block = position
        blocks = local_tiles
    else:
        inside = (windows >= 0) & (position >= start) & (position < start + size) & ~own
        block = (safe // local_tiles) * size + jnp.clip(position - start, 0, size - 1)
        blocks = (tile_count // local_tiles) * size
    order = jnp.argsort(jnp.logical_not(inside).astype(jnp.int32), axis=1, stable=True)
    ids = jnp.take_along_axis(block, order, axis=1)
    counts = jnp.sum(inside.astype(jnp.int32), axis=1)
    last = jnp.take_along_axis(ids, jnp.maximum(counts - 1, 0)[:, None], axis=1)
    slot = lax.broadcasted_iota(jnp.int32, ids.shape, 1)
    ids = jnp.where(slot < counts[:, None], ids, last)
    ids = jnp.clip(ids, 0, blocks - 1)
    return ids.reshape(-1).astype(jnp.int32), counts.astype(jnp.int32)


def phase_bound(local_tiles, tile_count, start, size, local=False):
    per_frame = FRAME_ROWS * FRAME_COLS
    frames = tile_count // per_frame
    best = 0
    for i in range(tile_count):
        fi, ri, ci = i // per_frame, i // FRAME_COLS % FRAME_ROWS, i % FRAME_COLS
        total = 0
        for fj in (fi - 1, fi, fi + 1):
            if not 0 <= fj < frames:
                continue
            near = 0
            for j in range(fj * per_frame, (fj + 1) * per_frame):
                rj, cj = j // FRAME_COLS % FRAME_ROWS, j % FRAME_COLS
                if local:
                    chosen = j // local_tiles == i // local_tiles
                else:
                    chosen = start <= j % local_tiles < start + size
                if abs(ri - rj) <= 2 and abs(ci - cj) <= 2 and chosen:
                    near += 1
            total += min(FRAME_SLOTS, near)
        best = max(best, total)
    return max(1, min(WINDOW_SLOTS, best))


def phase_sizes(local_tiles):
    if local_tiles % 2 == 0 and local_tiles >= 4:
        return [2] * (local_tiles // 2 - 1) + [1, 1]
    return [local_tiles]


def head_sums(partial, head_count):
    if head_count & (head_count - 1):
        return lax.psum(partial, "head")
    step = 1
    while step < head_count:
        pairs = [(i, i ^ step) for i in range(head_count)]
        partial = partial + lax.ppermute(partial, "head", pairs)
        step *= 2
    return partial


def on_device(query_states, key_states, value_states, query_gain, key_gain, windows, tok_count, head_count):
    rows = query_states.shape[0]
    local_tiles = rows // TILE_TOKENS
    tile_count = tok_count * local_tiles
    sizes = phase_sizes(local_tiles)
    key_total = head_sums(square_sums(key_states), head_count)
    sent_keys = normalize_rows(key_states, key_total, key_gain)
    query_in, _ = lax.optimization_barrier((query_states, sent_keys))
    query_total = head_sums(square_sums(query_in), head_count)
    query_normed = normalize_rows(query_in, query_total, query_gain)
    query_t = query_normed.T
    shard = lax.axis_index("tok")
    own = jnp.stack([sent_keys, value_states])
    ids, counts = phase_windows(windows, local_tiles, 0, local_tiles, tile_count, shard, True)
    bound = phase_bound(local_tiles, tile_count, 0, local_tiles, local=True)
    state = window_attention(query_t, own, ids, counts, None, False, bound)
    start = 0
    for number, size in enumerate(sizes):
        part = slice(start * TILE_TOKENS, (start + size) * TILE_TOKENS)
        paired = jnp.stack([sent_keys[part], value_states[part]])
        extended = lax.all_gather(paired, "tok", axis=1, tiled=True)
        ids, counts = phase_windows(windows, local_tiles, start, size, tile_count, shard, False)
        bound = phase_bound(local_tiles, tile_count, start, size)
        state = window_attention(
            query_t, extended, ids, counts, state, number == len(sizes) - 1, bound
        )
        start += size
    return state


def solution(mesh):
    in_specs = (
        P("tok", "head"),
        P("tok", "head"),
        P("tok", "head"),
        P("head"),
        P("head"),
        P("tok", None),
    )
    out_specs = P("tok", "head")
    return jax.shard_map(
        functools.partial(
            on_device, tok_count=mesh.shape["tok"], head_count=mesh.shape["head"]
        ),
        mesh=mesh,
        in_specs=in_specs,
        out_specs=out_specs,
        check_vma=False,
    )
```

```python
import functools
import math

import jax
import jax.numpy as jnp
from jax import lax
from jax.experimental import pallas as pl
from jax.experimental.pallas import tpu as pltpu
from jax.sharding import PartitionSpec as P

HEAD_DIM = 128
MODEL_DIM = 3072
TILE_TOKENS = 256
WINDOW_SLOTS = 27
LOG2_E = 1.4426950408889634
FRAME_SLOTS = 9
FRAME_ROWS = 4
FRAME_COLS = 4
SLOTS_PER_STEP = 1
STATS_HALF = 64


def square_sums(source):
    widened = source.astype(jnp.float32)
    return jnp.sum(widened * widened, axis=1)


def normalize_rows(source, totals, scale_gain):
    widened = source.astype(jnp.float32)
    return (widened * lax.rsqrt(totals[:, None] / MODEL_DIM + 1e-06) * scale_gain).astype(
        jnp.bfloat16
    )


def compact_windows(windows, tile_count):
    valid = windows >= 0
    order = jnp.argsort(jnp.logical_not(valid).astype(jnp.int32), axis=1, stable=True)
    ids = jnp.take_along_axis(windows, order, axis=1)
    counts = jnp.sum(valid.astype(jnp.int32), axis=1)
    last = jnp.take_along_axis(ids, jnp.maximum(counts - 1, 0)[:, None], axis=1)
    slot = lax.broadcasted_iota(jnp.int32, ids.shape, 1)
    ids = jnp.where(slot < counts[:, None], ids, last)
    ids = jnp.clip(ids, 0, tile_count - 1)
    return ids.reshape(-1).astype(jnp.int32), counts.astype(jnp.int32)


def attention_kernel(ids_ref, cnt_ref, q_ref, *refs, first, last):
    k_refs = refs[:SLOTS_PER_STEP]
    v_refs = refs[SLOTS_PER_STEP:2 * SLOTS_PER_STEP]
    rest = refs[2 * SLOTS_PER_STEP:]
    if not first:
        acc_in, stats_in = rest[:2]
        rest = rest[2:]
    if last:
        o_ref = rest[0]
        rest = rest[1:]
    else:
        acc_out, stats_out = rest[:2]
        rest = rest[2:]
    m_sc, l_sc, acc_sc = rest
    t = pl.program_id(0)
    j = pl.program_id(1)
    heads = q_ref.shape[0] // HEAD_DIM
    score_scale = 1.0 / math.sqrt(HEAD_DIM)

    @pl.when(j == 0)
    def _init():
        if first:
            m_sc[...] = jnp.full(m_sc.shape, -jnp.inf, jnp.float32)
            l_sc[...] = jnp.zeros(l_sc.shape, jnp.float32)
            acc_sc[...] = jnp.zeros(acc_sc.shape, jnp.float32)
        else:
            m_sc[...] = stats_in[0, 0]
            l_sc[...] = stats_in[0, 1]
            acc_sc[...] = acc_in[0]

    for sub in range(SLOTS_PER_STEP):
        k_ref = k_refs[sub]
        v_ref = v_refs[sub]

        @pl.when(j * SLOTS_PER_STEP + sub < cnt_ref[t])
        def _step():
            for h in range(heads):
                cols = slice(h * HEAD_DIM, (h + 1) * HEAD_DIM)
                q_t = q_ref[cols, :]
                k = k_ref[0, :, cols]
                v = v_ref[0, :, cols]
                scores = (
                    lax.dot_general(
                        k, q_t, (((1,), (0,)), ((), ())), preferred_element_type=jnp.float32
                    )
                    * (score_scale * LOG2_E)
                )
                m_prev = m_sc[h]
                m_cur = jnp.max(scores, axis=0, keepdims=True)
                m_new = jnp.maximum(m_prev, m_cur)
                alpha = jnp.exp2(m_prev - m_new)
                weights = jnp.exp2(scores - m_new)
                l_sc[h] = alpha * l_sc[h] + jnp.sum(weights, axis=0, keepdims=True)
                m_sc[h] = m_new
                mixed = lax.dot_general(
                    v, weights.astype(jnp.bfloat16), (((0,), (0,)), ((), ())),
                    preferred_element_type=jnp.float32,
                )
                acc_sc[cols, :] = acc_sc[cols, :] * alpha + mixed

    @pl.when(j == pl.num_programs(1) - 1)
    def _finish():
        if last:
            for h in range(heads):
                cols = slice(h * HEAD_DIM, (h + 1) * HEAD_DIM)
                o_ref[:, cols] = (acc_sc[cols, :] / l_sc[h]).T.astype(o_ref.dtype)
        else:
            acc_out[0] = acc_sc[...]
            stats_out[0, 0] = m_sc[...]
            stats_out[0, 1] = l_sc[...]


def window_attention(query_t, paired, ids, counts, state, last, bound):
    width, rows = query_t.shape
    local_tiles = rows // TILE_TOKENS
    heads = width // HEAD_DIM
    steps = bound // SLOTS_PER_STEP
    first = state is None

    def window_spec(lead, sub):
        return pl.BlockSpec(
            (1, TILE_TOKENS, width),
            lambda t, j, ids, cnt: (lead, ids[t * WINDOW_SLOTS + j * SLOTS_PER_STEP + sub], 0),
        )

    acc_spec = pl.BlockSpec((1, width, TILE_TOKENS), lambda t, j, ids, cnt: (t, 0, 0))
    stats_spec = pl.BlockSpec(
        (1, 2, heads, 1, TILE_TOKENS), lambda t, j, ids, cnt: (t, 0, 0, 0, 0)
    )
    in_specs = [pl.BlockSpec((width, TILE_TOKENS), lambda t, j, ids, cnt: (0, t))]
    in_specs += [window_spec(0, sub) for sub in range(SLOTS_PER_STEP)]
    in_specs += [window_spec(1, sub) for sub in range(SLOTS_PER_STEP)]
    operands = [ids, counts, query_t] + [paired] * (2 * SLOTS_PER_STEP)
    if not first:
        in_specs += [acc_spec, stats_spec]
        operands += list(state)
    if last:
        out_specs = pl.BlockSpec((TILE_TOKENS, width), lambda t, j, ids, cnt: (t, 0))
        out_shape = jax.ShapeDtypeStruct((rows, width), jnp.bfloat16)
    else:
        out_specs = [acc_spec, stats_spec]
        out_shape = [
            jax.ShapeDtypeStruct((local_tiles, width, TILE_TOKENS), jnp.float32),
            jax.ShapeDtypeStruct((local_tiles, 2, heads, 1, TILE_TOKENS), jnp.float32),
        ]
    grid_spec = pltpu.PrefetchScalarGridSpec(
        num_scalar_prefetch=2,
        grid=(local_tiles, steps),
        in_specs=in_specs,
        out_specs=out_specs,
        scratch_shapes=[
            pltpu.VMEM((heads, 1, TILE_TOKENS), jnp.float32),
            pltpu.VMEM((heads, 1, TILE_TOKENS), jnp.float32),
            pltpu.VMEM((width, TILE_TOKENS), jnp.float32),
        ],
    )
    return pl.pallas_call(
        functools.partial(attention_kernel, first=first, last=last),
        grid_spec=grid_spec,
        out_shape=out_shape,
        compiler_params=pltpu.CompilerParams(
            dimension_semantics=("arbitrary", "arbitrary")
        ),
    )(*operands)


def phase_windows(windows, local_tiles, start, size, tile_count, shard, local):
    safe = jnp.clip(windows, 0, tile_count - 1)
    position = safe % local_tiles
    own = safe // local_tiles == shard
    if local:
        inside = (windows >= 0) & own
        block = position
        blocks = local_tiles
    else:
        inside = (windows >= 0) & (position >= start) & (position < start + size) & ~own
        block = (safe // local_tiles) * size + jnp.clip(position - start, 0, size - 1)
        blocks = (tile_count // local_tiles) * size
    order = jnp.argsort(jnp.logical_not(inside).astype(jnp.int32), axis=1, stable=True)
    ids = jnp.take_along_axis(block, order, axis=1)
    counts = jnp.sum(inside.astype(jnp.int32), axis=1)
    last = jnp.take_along_axis(ids, jnp.maximum(counts - 1, 0)[:, None], axis=1)
    slot = lax.broadcasted_iota(jnp.int32, ids.shape, 1)
    ids = jnp.where(slot < counts[:, None], ids, last)
    ids = jnp.clip(ids, 0, blocks - 1)
    return ids.reshape(-1).astype(jnp.int32), counts.astype(jnp.int32)


def phase_bound(local_tiles, tile_count, start, size, local=False):
    per_frame = FRAME_ROWS * FRAME_COLS
    frames = tile_count // per_frame
    best = 0
    for i in range(tile_count):
        fi, ri, ci = i // per_frame, i // FRAME_COLS % FRAME_ROWS, i % FRAME_COLS
        total = 0
        for fj in (fi - 1, fi, fi + 1):
            if not 0 <= fj < frames:
                continue
            near = 0
            for j in range(fj * per_frame, (fj + 1) * per_frame):
                rj, cj = j // FRAME_COLS % FRAME_ROWS, j % FRAME_COLS
                if local:
                    chosen = j // local_tiles == i // local_tiles
                else:
                    chosen = start <= j % local_tiles < start + size
                if abs(ri - rj) <= 2 and abs(ci - cj) <= 2 and chosen:
                    near += 1
            total += min(FRAME_SLOTS, near)
        best = max(best, total)
    return max(1, min(WINDOW_SLOTS, best))


def phase_sizes(local_tiles):
    if local_tiles == 6:
        return [3, 2, 1]
    if local_tiles % 2 == 0 and local_tiles >= 4:
        return [2] * (local_tiles // 2 - 1) + [1, 1]
    return [local_tiles]


def head_sums(partial, head_count):
    if head_count & (head_count - 1):
        return lax.psum(partial, "head")
    step = 1
    while step < head_count:
        pairs = [(i, i ^ step) for i in range(head_count)]
        partial = partial + lax.ppermute(partial, "head", pairs)
        step *= 2
    return partial


def on_device(query_states, key_states, value_states, query_gain, key_gain, windows, tok_count, head_count):
    rows = query_states.shape[0]
    local_tiles = rows // TILE_TOKENS
    tile_count = tok_count * local_tiles
    sizes = phase_sizes(local_tiles)
    key_total = head_sums(square_sums(key_states), head_count)
    sent_keys = normalize_rows(key_states, key_total, key_gain)
    query_in, _ = lax.optimization_barrier((query_states, sent_keys))
    query_total = head_sums(square_sums(query_in), head_count)
    query_normed = normalize_rows(query_in, query_total, query_gain)
    query_t = query_normed.T
    shard = lax.axis_index("tok")
    own = jnp.stack([sent_keys, value_states])
    ids, counts = phase_windows(windows, local_tiles, 0, local_tiles, tile_count, shard, True)
    bound = phase_bound(local_tiles, tile_count, 0, local_tiles, local=True)
    state = window_attention(query_t, own, ids, counts, None, False, bound)
    start = 0
    for number, size in enumerate(sizes):
        part = slice(start * TILE_TOKENS, (start + size) * TILE_TOKENS)
        paired = jnp.stack([sent_keys[part], value_states[part]])
        extended = lax.all_gather(paired, "tok", axis=1, tiled=True)
        ids, counts = phase_windows(windows, local_tiles, start, size, tile_count, shard, False)
        bound = phase_bound(local_tiles, tile_count, start, size)
        state = window_attention(
            query_t, extended, ids, counts, state, number == len(sizes) - 1, bound
        )
        start += size
    return state


def solution(mesh):
    in_specs = (
        P("tok", "head"),
        P("tok", "head"),
        P("tok", "head"),
        P("head"),
        P("head"),
        P("tok", None),
    )
    out_specs = P("tok", "head")
    return jax.shard_map(
        functools.partial(
            on_device, tok_count=mesh.shape["tok"], head_count=mesh.shape["head"]
        ),
        mesh=mesh,
        in_specs=in_specs,
        out_specs=out_specs,
        check_vma=False,
    )
```
